256 devices in a mesh: req: 32 (over x, z), mlp: 8 (over y, core).
Axes of the slice: x: 4, y: 4, z: 8, core: 2. Of those that a mesh axis runs over, the one named last changes fastest.
Arguments:
- x_pages: bfloat16 [1024, 8, 4096], P('req', None, 'mlp'), may hold values from -6 to 6
- page_owner: int32 [1024], P('req'), may hold values from 0 to 31, as said below
- request_id: int32 [8192], P('req'), may hold values from 0 to 8191, as said below
- adapter_table: int32 [8192], P('req'), may hold values from 0 to 63
- ln_gain: float32 [4096], replicated, may hold values from 0.5 to 1.5
- ln_bias: float32 [4096], replicated, may hold values from -3 to 3
- w_query: bfloat16 [4096, 2048], P('req', 'mlp'), may hold values from -0.09375 to 0.09375
- w_key: bfloat16 [4096, 2048], P('req', 'mlp'), may hold values from -0.09375 to 0.09375
- w_value: bfloat16 [4096, 2048], P('req', 'mlp'), may hold values from -0.09375 to 0.09375
- w_attn_out: bfloat16 [2048, 4096], P('mlp', 'req'), may hold values from -0.125 to 0.125
- down_query: bfloat16 [4096, 1024], P('mlp'), may hold values from -0.09375 to 0.09375
- up_query: bfloat16 [1024, 2048], P(None, 'mlp'), may hold values from -1.5 to 1.5
- down_value: bfloat16 [4096, 1024], P('mlp'), may hold values from -0.09375 to 0.09375
- up_value: bfloat16 [1024, 2048], P(None, 'mlp'), may hold values from -1.5 to 1.5
- w_fc_in: bfloat16 [4096, 8192], P('req', 'mlp'), may hold values from -0.09375 to 0.09375
- b_fc_in: float32 [8192], P('mlp'), may hold values from -3 to 3
- down_fc: bfloat16 [4096, 1024], P('mlp'), may hold values from -0.09375 to 0.09375
- up_fc: bfloat16 [1024, 8192], P(None, 'mlp'), may hold values from -1.5 to 1.5
- w_fc_out: bfloat16 [8192, 4096], P('mlp', 'req'), may hold values from -0.0625 to 0.0625
- b_fc_out: float32 [4096], P('mlp'), may hold values from -3 to 3
Outputs:
- out_pages: bfloat16 [1024, 8, 4096], P('req', None, 'mlp')
The draws below stay inside these ranges and needn't reach their ends.
Inputs may be any that keep to these rules, and one draw needn't show every extreme that they name: `page_owner`: every owner receives exactly 32 pages, at most 2 of them from one device, and some device sends exactly 2 pages to some owner. `request_id`: ids never fall; every request lies inside one owner's block of 256 rows, and the ids of block k lie in k * 256 to k * 256 + 255; some request is 256 long.
All inputs are finite; a program needn't handle non-finite values.
Results may differ from the reference program's by a relative error of at most 0.006.
Values may be sent and summed in bfloat16 or wider, within the bound.
No kernel may reach another device: no remote copies, remote signals or barrier semaphores. Data moves between devices by JAX's collectives and lax.ppermute only.
A program may use at most 128 MiB of HBM per device.

```python
import math
import jax
import jax.numpy as jnp
import numpy as np
from jax import lax

D = 4096
HEADS = 8
HS = 256
ROT = 64
FF = 8192
NAD = 64
R = 16
PAGE = 8
TOK_DEV = 256
HW = 2048
PG_DEV = 32
PAGES = 1024
TOKENS = 8192
N_REQ = 32


def draw_request_id(key, part):
    blocks = TOKENS // TOK_DEV
    key_level = jax.random.fold_in(key, 11)
    key_flag = jax.random.fold_in(key, 12)
    key_long = jax.random.fold_in(key, 13)
    level = jax.random.randint(key_level, (blocks, 1), 1, 5)
    period = jnp.power(4, level).astype(jnp.int32)
    raw = jax.random.randint(key_flag, (blocks, TOK_DEV), 0, 1 << 20)
    flags = (raw % period == 0).astype(jnp.int32)
    column = jnp.arange(TOK_DEV)[None, :]
    long_block = jax.random.randint(key_long, (), 0, blocks)
    flags = jnp.where(column == 0, 1, flags)
    flags = jnp.where((jnp.arange(blocks)[:, None] == long_block) & (column > 0), 0, flags)
    ids = jnp.cumsum(flags, axis=1) - 1 + jnp.arange(blocks)[:, None] * TOK_DEV
    return ids.reshape(-1).astype(jnp.int32)


def draw_page_owner(key, part):
    groups = N_REQ
    per = PG_DEV
    base = per // groups
    key_sign = jax.random.fold_in(key, 21)
    key_rows = jax.random.fold_in(key, 22)
    signs = jnp.where(jax.random.permutation(key_sign, groups) < groups // 2, 1, -1).astype(jnp.int32)
    residue = jnp.arange(groups)

    def one_source(source):
        counts = base + signs[(residue + 2 * source) % groups]
        offsets = jnp.repeat(residue, counts, total_repeat_length=per)
        shuffle = jax.random.permutation(jax.random.fold_in(key_rows, source), per)
        return ((source + offsets[shuffle]) % groups).astype(jnp.int32)
    owners = jax.vmap(one_source)(jnp.arange(groups))
    return owners.reshape(-1).astype(jnp.int32)


def set_ends(drawn, key, smallest, high):
    place = [jax.random.randint(jax.random.fold_in(key, axis), (), 0, length) for axis, length in enumerate(drawn.shape)]
    longest = drawn.shape.index(max(drawn.shape))
    neighbour = place[:longest] + [(place[longest] + 1) % drawn.shape[longest]] + place[longest + 1:]
    return drawn.at[tuple(place)].set(smallest).at[tuple(neighbour)].set(high)


def level_of(rng, shape, pieces, smallest, high):
    factor_of, own = 1.0, jax.random.fold_in(rng, 6)
    for dim, shards_of in pieces:
        draws = jnp.exp(jax.random.uniform(jax.random.fold_in(own, dim), (shards_of,), jnp.float32, smallest / len(pieces), high / len(pieces)))
        factor_of = factor_of * jnp.repeat(draws, shape[dim] // shards_of).reshape([-1 if axis == dim else 1 for axis in range(len(shape))])
    return factor_of


def rank_bounds(count, lean):
    loads = [(1 << 20) // math.isqrt(grade ** lean) + 1 for grade in range(1, count + 1)]
    width = 1 + sum(loads) // (1 << 30)
    return np.cumsum(np.array([max(1, weight // width) for weight in loads]))


def skewed_ids(key, extent, count, skew):
    listing = rank_bounds(count, skew)
    ticket = jax.random.randint(jax.random.fold_in(key, 1), extent, 0, int(listing[count - 1]))
    standing = jnp.searchsorted(jnp.asarray(listing, jnp.int32), ticket, side="right")
    return jax.random.permutation(jax.random.fold_in(key, 2), count)[standing].astype(jnp.int32)


def noise(stream_key, shape, deviation, bound, split=(), kind=jnp.bfloat16):
    drawn = jax.random.normal(stream_key, shape, jnp.float32) * deviation
    if len(split) > 0:
        drawn = level_of(stream_key, shape, split, -0.22, 0.18) * drawn
    return jnp.clip(drawn, min=-bound, max=bound).astype(kind)


def setup_inputs(seed: int = 0) -> dict:
    arg_keys = jax.random.split(jax.random.key(seed), 21)
    return {
        "x_pages": noise(arg_keys[0], (PAGES, PAGE, D), 1.0, 6.0, ((0, 32), (2, 8))),
        "page_owner": draw_page_owner(jax.random.fold_in(arg_keys[20], 71), 0),
        "request_id": draw_request_id(jax.random.fold_in(arg_keys[20], 71), 0),
        "adapter_table": set_ends(skewed_ids(arg_keys[3], (TOKENS,), NAD, 2), jax.random.fold_in(arg_keys[3], 3), 0, NAD - 1).astype(jnp.int32),
        "ln_gain": jnp.clip(1.0 + 0.1 * jax.random.normal(arg_keys[4], (D,), jnp.float32), 0.5, 1.5),
        "ln_bias": noise(arg_keys[5], (D,), 0.3, 3.0, (), jnp.float32),
        "w_query": noise(arg_keys[6], (D, HW), D ** -0.5, 0.09375, ((0, 32), (1, 8))),
        "w_key": noise(arg_keys[7], (D, HW), D ** -0.5, 0.09375, ((0, 32), (1, 8))),
        "w_value": noise(arg_keys[8], (D, HW), D ** -0.5, 0.09375, ((0, 32), (1, 8))),
        "w_attn_out": noise(arg_keys[9], (HW, D), HW ** -0.5, 0.125, ((0, 8), (1, 32))),
        "down_query": noise(arg_keys[10], (D, NAD * R), D ** -0.5, 0.09375, ((0, 8),)),
        "up_query": noise(arg_keys[11], (NAD * R, HW), R ** -0.5, 1.5, ((1, 8),)),
        "down_value": noise(arg_keys[12], (D, NAD * R), D ** -0.5, 0.09375, ((0, 8),)),
        "up_value": noise(arg_keys[13], (NAD * R, HW), R ** -0.5, 1.5, ((1, 8),)),
        "w_fc_in": noise(arg_keys[14], (D, FF), D ** -0.5, 0.09375, ((0, 32), (1, 8))),
        "b_fc_in": noise(arg_keys[15], (FF,), 0.5, 3.0, ((0, 8),), jnp.float32),
        "down_fc": noise(arg_keys[16], (D, NAD * R), D ** -0.5, 0.09375, ((0, 8),)),
        "up_fc": noise(arg_keys[17], (NAD * R, FF), R ** -0.5, 1.5, ((1, 8),)),
        "w_fc_out": noise(arg_keys[18], (FF, D), FF ** -0.5, 0.0625, ((0, 8), (1, 32))),
        "b_fc_out": noise(arg_keys[19], (D,), 0.5, 3.0, ((0, 8),), jnp.float32),
    }


EPS = 1e-05

def gelu_tanh(v):
    return 0.5 * v * (1.0 + jnp.tanh(0.7978845608028654 * (v + 0.044715 * v * v * v)))

def rotate(block, pos):
    half = ROT // 2
    freq = jnp.power(10000.0, -jnp.arange(half).astype(jnp.float32) * 2.0 / ROT)
    angle = pos.astype(jnp.float32)[:, None, None] * freq[None, None, :]
    cosine = jnp.cos(angle)
    sine = jnp.sin(angle)
    even = block[:, :, 0:ROT:2]
    odd = block[:, :, 1:ROT:2]
    turned = jnp.stack([even * cosine - odd * sine, odd * cosine + even * sine], axis=-1)
    turned = turned.reshape(block.shape[0], block.shape[1], ROT)
    return jnp.concatenate([turned, block[:, :, ROT:]], axis=2)

def low_rank(normed, down, up, onehot):
    rows = normed.shape[0]
    spread = jnp.dot(normed, down, preferred_element_type=jnp.float32).reshape(rows, NAD, R)
    chosen = lax.optimization_barrier(jnp.sum(spread * onehot[:, :, None], axis=1)).astype(jnp.bfloat16)
    expanded = (onehot.astype(jnp.bfloat16)[:, :, None] * chosen[:, None, :]).reshape(rows, NAD * R)
    return jnp.dot(expanded, up, preferred_element_type=jnp.float32)

def reference(x_pages, page_owner, request_id, adapter_table, ln_gain, ln_bias, w_query, w_key, w_value, w_attn_out, down_query, up_query, down_value, up_value, w_fc_in, b_fc_in, down_fc, up_fc, w_fc_out, b_fc_out):
    order = jnp.argsort(page_owner, stable=True).astype(jnp.int32)
    moved = x_pages[order].reshape(N_REQ, TOK_DEV, D)
    owner_ids = request_id.reshape(N_REQ, TOK_DEV)

    def layer(item):
        rows, ids = item
        count = rows.shape[0]
        xf = rows.astype(jnp.float32)
        mean = lax.optimization_barrier(jnp.mean(xf, axis=1, keepdims=True))
        var = lax.optimization_barrier(jnp.mean(jnp.square(xf - mean), axis=1, keepdims=True))
        normed = ((xf - mean) * lax.rsqrt(var + EPS) * ln_gain + ln_bias).astype(jnp.bfloat16)
        adapter = adapter_table[ids]
        onehot = (adapter[:, None] == jnp.arange(NAD)[None, :]).astype(jnp.float32)
        index = jnp.arange(count)
        start = lax.optimization_barrier(jnp.sum((ids[None, :] < ids[:, None]).astype(jnp.int32), axis=1))
        pos = index - start
        query = jnp.dot(normed, w_query, preferred_element_type=jnp.float32) + low_rank(normed, down_query, up_query, onehot)
        keys = jnp.dot(normed, w_key, preferred_element_type=jnp.float32)
        value = (jnp.dot(normed, w_value, preferred_element_type=jnp.float32) + low_rank(normed, down_value, up_value, onehot)).astype(jnp.bfloat16)
        query = rotate(query.reshape(count, HEADS, HS), pos).astype(jnp.bfloat16)
        keys = rotate(keys.reshape(count, HEADS, HS), pos).astype(jnp.bfloat16)
        value = value.reshape(count, HEADS, HS)
        mask = (ids[:, None] == ids[None, :]) & (index[None, :] <= index[:, None])
        scores = jnp.einsum('qhd,khd->hqk', query.astype(jnp.float32), keys.astype(jnp.float32)) * HS ** (-0.5)
        scores = jnp.where(mask[None, :, :], scores, -1e+30)
        top = lax.optimization_barrier(jnp.max(scores, axis=2, keepdims=True))
        weights = jnp.exp(scores - top)
        probs = (weights / lax.optimization_barrier(jnp.sum(weights, axis=2, keepdims=True))).astype(jnp.bfloat16)
        attn = jnp.einsum('hqk,khd->qhd', probs.astype(jnp.float32), value.astype(jnp.float32)).astype(jnp.bfloat16).reshape(count, HW)
        hidden_pre = jnp.dot(normed, w_fc_in, preferred_element_type=jnp.float32) + low_rank(normed, down_fc, up_fc, onehot) + b_fc_in
        hidden = gelu_tanh(hidden_pre).astype(jnp.bfloat16)
        mixed = jnp.dot(attn, w_attn_out, preferred_element_type=jnp.float32) + jnp.dot(hidden, w_fc_out, preferred_element_type=jnp.float32)
        return (xf + mixed + b_fc_out).astype(jnp.bfloat16)
    result = lax.map(layer, (moved, owner_ids))
    back = jnp.argsort(order).astype(jnp.int32)
    return result.reshape(PAGES, PAGE, D)[back]
```

```python
import jax
import jax.numpy as jnp
from jax import lax
from jax.sharding import PartitionSpec as P

HS = 256
ROT = 64
NAD = 64
R = 16


EPS = 1e-05


def gelu_tanh(v):
    return 0.5 * v * (1.0 + jnp.tanh(0.7978845608028654 * (v + 0.044715 * v * v * v)))


def rotate(block, pos):
    half = ROT // 2
    freq = jnp.power(10000.0, -jnp.arange(half).astype(jnp.float32) * 2.0 / ROT)
    angle = pos.astype(jnp.float32)[:, None, None] * freq[None, None, :]
    cosine = jnp.cos(angle)
    sine = jnp.sin(angle)
    even = block[:, :, 0:ROT:2]
    odd = block[:, :, 1:ROT:2]
    turned = jnp.stack([even * cosine - odd * sine, odd * cosine + even * sine], axis=-1)
    turned = turned.reshape(block.shape[0], block.shape[1], ROT)
    return jnp.concatenate([turned, block[:, :, ROT:]], axis=2)


def on_device(
    x_pages,
    page_owner,
    request_id,
    adapter_table,
    ln_gain,
    ln_bias,
    w_query,
    w_key,
    w_value,
    w_attn_out,
    down_query,
    up_query,
    down_value,
    up_value,
    w_fc_in,
    b_fc_in,
    down_fc,
    up_fc,
    w_fc_out,
    b_fc_out,
):
    groups = lax.axis_size("req")
    pg_dev = x_pages.shape[0]
    page_len = x_pages.shape[1]
    width_m = x_pages.shape[2]
    tok = request_id.shape[0]
    per_owner = pg_dev // groups + 1
    slots = groups * per_owner
    page_iota = jnp.arange(pg_dev)
    earlier = (page_owner[None, :] == page_owner[:, None]) & (
        page_iota[None, :] < page_iota[:, None]
    )
    rank = jnp.sum(earlier.astype(jnp.int32), axis=1)
    slot = page_owner * per_owner + rank
    place = (slot[None, :] == jnp.arange(slots)[:, None]).astype(jnp.bfloat16)
    flat_pages = x_pages.reshape(pg_dev, page_len * width_m)
    outgoing = jnp.dot(place, flat_pages, preferred_element_type=jnp.float32).astype(jnp.bfloat16)
    outgoing = outgoing.reshape(groups, per_owner, page_len * width_m)
    filled = jnp.sum(place, axis=1).reshape(groups, per_owner)
    arrived, marks = (
        lax.all_to_all(outgoing, "req", split_axis=0, concat_axis=0, tiled=True),
        lax.all_to_all(filled, "req", split_axis=0, concat_axis=0, tiled=True),
    )
    valid = marks.reshape(slots).astype(jnp.float32)
    position = jnp.cumsum(valid) - 1.0
    take = (
        (position[None, :] == jnp.arange(pg_dev).astype(jnp.float32)[:, None])
        & (valid[None, :] > 0.5)
    ).astype(jnp.bfloat16)
    own_x = jnp.dot(
        take, arrived.reshape(slots, page_len * width_m), preferred_element_type=jnp.float32
    )
    own_x = own_x.astype(jnp.bfloat16).reshape(tok, width_m)
    column = lax.axis_index("mlp") * width_m
    whole = lax.all_gather(own_x, "mlp", axis=1, tiled=True).astype(jnp.float32)
    mean = jnp.mean(whole, axis=1, keepdims=True)
    var = jnp.mean(jnp.square(whole - mean), axis=1, keepdims=True)
    full_ln = ((whole - mean) * lax.rsqrt(var + EPS) * ln_gain + ln_bias).astype(jnp.bfloat16)
    ln_m = lax.dynamic_slice_in_dim(full_ln, column, width_m, 1)
    local_req = request_id - lax.axis_index("req") * tok
    lookup = local_req[:, None] == jnp.arange(tok)[None, :]
    adapter = jnp.sum(jnp.where(lookup, adapter_table[None, :], 0), axis=1)
    onehot = (adapter[:, None] == jnp.arange(NAD)[None, :]).astype(jnp.float32)
    onehot_low = onehot.astype(jnp.bfloat16)

    def pick(down):
        spread = jnp.dot(ln_m, down, preferred_element_type=jnp.float32).reshape(tok, NAD, R)
        return jnp.sum(spread * onehot[:, :, None], axis=1)

    picked = lax.psum((pick(down_query), pick(down_value), pick(down_fc)), "mlp")

    def lift(chosen, up):
        expanded = (onehot_low[:, :, None] * chosen.astype(jnp.bfloat16)[:, None, :]).reshape(
            tok, NAD * R
        )
        return jnp.dot(expanded, up, preferred_element_type=jnp.float32)

    row_iota = jnp.arange(tok)
    start = jnp.sum((request_id[None, :] < request_id[:, None]).astype(jnp.int32), axis=1)
    pos = row_iota - start
    mask = (request_id[:, None] == request_id[None, :]) & (row_iota[None, :] <= row_iota[:, None])
    heads_w = w_query.shape[1]
    ff_w = w_fc_in.shape[1]
    packed = jnp.concatenate(
        [w_query, w_key, w_value, w_fc_in, w_attn_out.T, w_fc_out.T], axis=1
    )
    gathered = lax.all_gather(packed, "req", axis=0, tiled=True)
    n_in = 3 * heads_w + ff_w
    base = jnp.dot(full_ln, gathered[:, :n_in], preferred_element_type=jnp.float32)
    base_q = base[:, :heads_w]
    base_k = base[:, heads_w : 2 * heads_w]
    base_v = base[:, 2 * heads_w : 3 * heads_w]
    query = rotate(
        (base_q + lift(picked[0], up_query)).reshape(tok, heads_w // HS, HS), pos
    ).astype(jnp.bfloat16)
    keys = rotate(base_k.reshape(tok, heads_w // HS, HS), pos).astype(jnp.bfloat16)
    value = (
        (base_v + lift(picked[1], up_value)).astype(jnp.bfloat16).reshape(tok, heads_w // HS, HS)
    )
    scores = jnp.einsum("qhd,khd->hqk", query, keys, preferred_element_type=jnp.float32) * HS ** (
        -0.5
    )
    scores = jnp.where(mask[None, :, :], scores, -1e30)
    top = jnp.max(scores, axis=2, keepdims=True)
    weights = jnp.exp(scores - top)
    probs = (weights / jnp.sum(weights, axis=2, keepdims=True)).astype(jnp.bfloat16)
    mixed_heads = jnp.einsum("hqk,khd->qhd", probs, value, preferred_element_type=jnp.float32)
    attn = mixed_heads.astype(jnp.bfloat16).reshape(tok, heads_w)
    hidden_pre = base[:, 3 * heads_w :]
    hidden_pre = hidden_pre + lift(picked[2], up_fc) + b_fc_in
    hidden = gelu_tanh(hidden_pre).astype(jnp.bfloat16)
    joined = jnp.concatenate([attn, hidden], axis=1)
    part = lax.dot_general(
        joined,
        gathered[:, n_in:],
        (((1,), (1,)), ((), ())),
        preferred_element_type=jnp.float32,
    )
    shares = lax.psum_scatter(part, "mlp", scatter_dimension=1, tiled=True)
    result = (own_x.astype(jnp.float32) + shares + b_fc_out).astype(jnp.bfloat16)
    back_flat = result.reshape(pg_dev, page_len * width_m)
    leaving = jnp.dot(take.T, back_flat, preferred_element_type=jnp.float32).astype(jnp.bfloat16)
    leaving = leaving.reshape(groups, per_owner, page_len * width_m)
    returned = lax.all_to_all(leaving, "req", split_axis=0, concat_axis=0, tiled=True)
    pages_back = jnp.dot(
        place.T, returned.reshape(slots, page_len * width_m), preferred_element_type=jnp.float32
    )
    return pages_back.astype(jnp.bfloat16).reshape(pg_dev, page_len, width_m)


def solution(mesh):
    in_specs = (
        P("req", None, "mlp"),
        P("req"),
        P("req"),
        P("req"),
        P(),
        P(),
        P("req", "mlp"),
        P("req", "mlp"),
        P("req", "mlp"),
        P("mlp", "req"),
        P("mlp", None),
        P(None, "mlp"),
        P("mlp", None),
        P(None, "mlp"),
        P("req", "mlp"),
        P("mlp"),
        P("mlp", None),
        P(None, "mlp"),
        P("mlp", "req"),
        P("mlp"),
    )
    out_specs = P("req", None, "mlp")
    return jax.shard_map(
        on_device, mesh=mesh, in_specs=in_specs, out_specs=out_specs, check_vma=False
    )
```

```python
import jax
import jax.numpy as jnp
from jax import lax
from jax.sharding import PartitionSpec as P

HS = 256
ROT = 64
NAD = 64
R = 16


EPS = 1e-05


def gelu_tanh(v):
    return 0.5 * v * (1.0 + jnp.tanh(0.7978845608028654 * (v + 0.044715 * v * v * v)))


def rotate(block, pos):
    half = ROT // 2
    freq = jnp.power(10000.0, -jnp.arange(half).astype(jnp.float32) * 2.0 / ROT)
    angle = pos.astype(jnp.float32)[:, None, None] * freq[None, None, :]
    cosine = jnp.cos(angle)
    sine = jnp.sin(angle)
    even = block[:, :, 0:ROT:2]
    odd = block[:, :, 1:ROT:2]
    turned = jnp.stack([even * cosine - odd * sine, odd * cosine + even * sine], axis=-1)
    turned = turned.reshape(block.shape[0], block.shape[1], ROT)
    return jnp.concatenate([turned, block[:, :, ROT:]], axis=2)


def on_device(
    x_pages,
    page_owner,
    request_id,
    adapter_table,
    ln_gain,
    ln_bias,
    w_query,
    w_key,
    w_value,
    w_attn_out,
    down_query,
    up_query,
    down_value,
    up_value,
    w_fc_in,
    b_fc_in,
    down_fc,
    up_fc,
    w_fc_out,
    b_fc_out,
):
    groups = lax.axis_size("req")
    pg_dev = x_pages.shape[0]
    page_len = x_pages.shape[1]
    width_m = x_pages.shape[2]
    tok = request_id.shape[0]
    per_owner = pg_dev // groups + 1
    slots = groups * per_owner
    page_iota = jnp.arange(pg_dev)
    earlier = (page_owner[None, :] == page_owner[:, None]) & (
        page_iota[None, :] < page_iota[:, None]
    )
    rank = jnp.sum(earlier.astype(jnp.int32), axis=1)
    slot = page_owner * per_owner + rank
    place = (slot[None, :] == jnp.arange(slots)[:, None]).astype(jnp.bfloat16)
    flat_pages = x_pages.reshape(pg_dev, page_len * width_m)
    outgoing = jnp.dot(place, flat_pages, preferred_element_type=jnp.float32).astype(jnp.bfloat16)
    outgoing = outgoing.reshape(groups, per_owner, page_len * width_m)
    filled = jnp.sum(place, axis=1).reshape(groups, per_owner)
    arrived, marks = (
        lax.all_to_all(outgoing, "req", split_axis=0, concat_axis=0, tiled=True),
        lax.all_to_all(filled, "req", split_axis=0, concat_axis=0, tiled=True),
    )
    valid = marks.reshape(slots).astype(jnp.float32)
    position = jnp.cumsum(valid) - 1.0
    take = (
        (position[None, :] == jnp.arange(pg_dev).astype(jnp.float32)[:, None])
        & (valid[None, :] > 0.5)
    ).astype(jnp.bfloat16)
    own_x = jnp.dot(
        take, arrived.reshape(slots, page_len * width_m), preferred_element_type=jnp.float32
    )
    own_x = own_x.astype(jnp.bfloat16).reshape(tok, width_m)
    column = lax.axis_index("mlp") * width_m
    n_mlp = lax.axis_size("mlp")
    copies = jnp.broadcast_to(own_x[None], (n_mlp, tok, width_m))
    spread_x = lax.all_to_all(copies, "mlp", split_axis=0, concat_axis=0, tiled=True)
    whole = jnp.transpose(spread_x, (1, 0, 2)).reshape(tok, n_mlp * width_m).astype(jnp.float32)
    mean = jnp.mean(whole, axis=1, keepdims=True)
    var = jnp.mean(jnp.square(whole - mean), axis=1, keepdims=True)
    full_ln = ((whole - mean) * lax.rsqrt(var + EPS) * ln_gain + ln_bias).astype(jnp.bfloat16)
    ln_m = lax.dynamic_slice_in_dim(full_ln, column, width_m, 1)
    local_req = request_id - lax.axis_index("req") * tok
    lookup = local_req[:, None] == jnp.arange(tok)[None, :]
    adapter = jnp.sum(jnp.where(lookup, adapter_table[None, :], 0), axis=1)
    onehot = (adapter[:, None] == jnp.arange(NAD)[None, :]).astype(jnp.float32)
    onehot_low = onehot.astype(jnp.bfloat16)

    def pick(down):
        spread = jnp.dot(ln_m, down, preferred_element_type=jnp.float32).reshape(tok, NAD, R)
        return jnp.sum(spread * onehot[:, :, None], axis=1)

    picked = lax.psum((pick(down_query), pick(down_value), pick(down_fc)), "mlp")

    def lift(chosen, up):
        expanded = (onehot_low[:, :, None] * chosen.astype(jnp.bfloat16)[:, None, :]).reshape(
            tok, NAD * R
        )
        return jnp.dot(expanded, up, preferred_element_type=jnp.float32)

    row_iota = jnp.arange(tok)
    start = jnp.sum((request_id[None, :] < request_id[:, None]).astype(jnp.int32), axis=1)
    pos = row_iota - start
    mask = (request_id[:, None] == request_id[None, :]) & (row_iota[None, :] <= row_iota[:, None])
    heads_w = w_query.shape[1]
    ff_w = w_fc_in.shape[1]
    packed = jnp.concatenate(
        [w_query, w_key, w_value, w_fc_in, w_attn_out.T, w_fc_out.T], axis=1
    )
    gathered = lax.all_gather(packed, "req", axis=0, tiled=True)
    n_in = 3 * heads_w + ff_w
    base = jnp.dot(full_ln, gathered[:, :n_in], preferred_element_type=jnp.float32)
    base_q = base[:, :heads_w]
    base_k = base[:, heads_w : 2 * heads_w]
    base_v = base[:, 2 * heads_w : 3 * heads_w]
    query = rotate(
        (base_q + lift(picked[0], up_query)).reshape(tok, heads_w // HS, HS), pos
    ).astype(jnp.bfloat16)
    keys = rotate(base_k.reshape(tok, heads_w // HS, HS), pos).astype(jnp.bfloat16)
    value = (
        (base_v + lift(picked[1], up_value)).astype(jnp.bfloat16).reshape(tok, heads_w // HS, HS)
    )
    scores = jnp.einsum("qhd,khd->hqk", query, keys, preferred_element_type=jnp.float32) * HS ** (
        -0.5
    )
    scores = jnp.where(mask[None, :, :], scores, -1e30)
    top = jnp.max(scores, axis=2, keepdims=True)
    weights = jnp.exp(scores - top)
    probs = (weights / jnp.sum(weights, axis=2, keepdims=True)).astype(jnp.bfloat16)
    mixed_heads = jnp.einsum("hqk,khd->qhd", probs, value, preferred_element_type=jnp.float32)
    attn = mixed_heads.astype(jnp.bfloat16).reshape(tok, heads_w)
    hidden_pre = base[:, 3 * heads_w :]
    hidden_pre = hidden_pre + lift(picked[2], up_fc) + b_fc_in
    hidden = gelu_tanh(hidden_pre).astype(jnp.bfloat16)
    joined = jnp.concatenate([attn, hidden], axis=1)
    part = lax.dot_general(
        joined,
        gathered[:, n_in:],
        (((1,), (1,)), ((), ())),
        preferred_element_type=jnp.float32,
    )
    shares = lax.psum_scatter(part, "mlp", scatter_dimension=1, tiled=True)
    result = (own_x.astype(jnp.float32) + shares + b_fc_out).astype(jnp.bfloat16)
    back_flat = result.reshape(pg_dev, page_len * width_m)
    leaving = jnp.dot(take.T, back_flat, preferred_element_type=jnp.float32).astype(jnp.bfloat16)
    leaving = leaving.reshape(groups, per_owner, page_len * width_m)
    returned = lax.all_to_all(leaving, "req", split_axis=0, concat_axis=0, tiled=True)
    pages_back = jnp.dot(
        place.T, returned.reshape(slots, page_len * width_m), preferred_element_type=jnp.float32
    )
    return pages_back.astype(jnp.bfloat16).reshape(pg_dev, page_len, width_m)


def solution(mesh):
    in_specs = (
        P("req", None, "mlp"),
        P("req"),
        P("req"),
        P("req"),
        P(),
        P(),
        P("req", "mlp"),
        P("req", "mlp"),
        P("req", "mlp"),
        P("mlp", "req"),
        P("mlp", None),
        P(None, "mlp"),
        P("mlp", None),
        P(None, "mlp"),
        P("req", "mlp"),
        P("mlp"),
        P("mlp", None),
        P(None, "mlp"),
        P("mlp", "req"),
        P("mlp"),
    )
    out_specs = P("req", None, "mlp")
    return jax.shard_map(
        on_device, mesh=mesh, in_specs=in_specs, out_specs=out_specs, check_vma=False
    )
```

```python
import jax
import jax.numpy as jnp
from jax import lax
from jax.sharding import PartitionSpec as P

HS = 256
ROT = 64
NAD = 64
R = 16


EPS = 1e-05


def gelu_tanh(v):
    return 0.5 * v * (1.0 + jnp.tanh(0.7978845608028654 * (v + 0.044715 * v * v * v)))


def rotate(block, pos):
    half = ROT // 2
    freq = jnp.power(10000.0, -jnp.arange(half).astype(jnp.float32) * 2.0 / ROT)
    angle = pos.astype(jnp.float32)[:, None, None] * freq[None, None, :]
    cosine = jnp.cos(angle)
    sine = jnp.sin(angle)
    even = block[:, :, 0:ROT:2]
    odd = block[:, :, 1:ROT:2]
    turned = jnp.stack([even * cosine - odd * sine, odd * cosine + even * sine], axis=-1)
    turned = turned.reshape(block.shape[0], block.shape[1], ROT)
    return jnp.concatenate([turned, block[:, :, ROT:]], axis=2)


def on_device(
    x_pages,
    page_owner,
    request_id,
    adapter_table,
    ln_gain,
    ln_bias,
    w_query,
    w_key,
    w_value,
    w_attn_out,
    down_query,
    up_query,
    down_value,
    up_value,
    w_fc_in,
    b_fc_in,
    down_fc,
    up_fc,
    w_fc_out,
    b_fc_out,
):
    groups = lax.axis_size("req")
    pg_dev = x_pages.shape[0]
    page_len = x_pages.shape[1]
    width_m = x_pages.shape[2]
    tok = request_id.shape[0]
    per_owner = pg_dev // groups + 1
    slots = groups * per_owner
    page_iota = jnp.arange(pg_dev)
    earlier = (page_owner[None, :] == page_owner[:, None]) & (
        page_iota[None, :] < page_iota[:, None]
    )
    rank = jnp.sum(earlier.astype(jnp.int32), axis=1)
    slot = page_owner * per_owner + rank
    place = (slot[None, :] == jnp.arange(slots)[:, None]).astype(jnp.bfloat16)
    flat_pages = x_pages.reshape(pg_dev, page_len * width_m)
    outgoing = jnp.dot(place, flat_pages, preferred_element_type=jnp.float32).astype(jnp.bfloat16)
    outgoing = outgoing.reshape(groups, per_owner, page_len * width_m)
    filled = jnp.sum(place, axis=1).reshape(groups, per_owner)
    arrived, marks = (
        lax.all_to_all(outgoing, "req", split_axis=0, concat_axis=0, tiled=True),
        lax.all_to_all(filled, "req", split_axis=0, concat_axis=0, tiled=True),
    )
    valid = marks.reshape(slots).astype(jnp.float32)
    position = jnp.cumsum(valid) - 1.0
    take = (
        (position[None, :] == jnp.arange(pg_dev).astype(jnp.float32)[:, None])
        & (valid[None, :] > 0.5)
    ).astype(jnp.bfloat16)
    own_x = jnp.dot(
        take, arrived.reshape(slots, page_len * width_m), preferred_element_type=jnp.float32
    )
    own_x = own_x.astype(jnp.bfloat16).reshape(tok, width_m)
    column = lax.axis_index("mlp") * width_m
    n_mlp = lax.axis_size("mlp")
    copies = jnp.broadcast_to(own_x[None], (n_mlp, tok, width_m))
    spread_x = lax.all_to_all(copies, "mlp", split_axis=0, concat_axis=0, tiled=True)
    whole = jnp.transpose(spread_x, (1, 0, 2)).reshape(tok, n_mlp * width_m).astype(jnp.float32)
    mean = jnp.mean(whole, axis=1, keepdims=True)
    var = jnp.mean(jnp.square(whole - mean), axis=1, keepdims=True)
    full_ln = ((whole - mean) * lax.rsqrt(var + EPS) * ln_gain + ln_bias).astype(jnp.bfloat16)
    ln_m = lax.dynamic_slice_in_dim(full_ln, column, width_m, 1)
    local_req = request_id - lax.axis_index("req") * tok
    lookup = local_req[:, None] == jnp.arange(tok)[None, :]
    adapter = jnp.sum(jnp.where(lookup, adapter_table[None, :], 0), axis=1)
    onehot = (adapter[:, None] == jnp.arange(NAD)[None, :]).astype(jnp.float32)
    onehot_low = onehot.astype(jnp.bfloat16)

    def pick(down):
        spread = jnp.dot(ln_m, down, preferred_element_type=jnp.float32).reshape(tok, NAD, R)
        return jnp.sum(spread * onehot[:, :, None], axis=1)

    picked = lax.psum((pick(down_query), pick(down_value), pick(down_fc)), "mlp")

    def lift(chosen, up):
        expanded = (onehot_low[:, :, None] * chosen.astype(jnp.bfloat16)[:, None, :]).reshape(
            tok, NAD * R
        )
        return jnp.dot(expanded, up, preferred_element_type=jnp.float32)

    row_iota = jnp.arange(tok)
    start = jnp.sum((request_id[None, :] < request_id[:, None]).astype(jnp.int32), axis=1)
    pos = row_iota - start
    mask = (request_id[:, None] == request_id[None, :]) & (row_iota[None, :] <= row_iota[:, None])
    heads_w = w_query.shape[1]
    ff_w = w_fc_in.shape[1]
    packed = jnp.concatenate([w_query, w_key, w_value, w_fc_in, w_attn_out.T], axis=1)
    fo_copies = jnp.broadcast_to(w_fc_out[None], (groups,) + w_fc_out.shape)
    fo_rows = lax.all_to_all(fo_copies, "req", split_axis=0, concat_axis=0, tiled=True)
    gathered = lax.all_gather(packed, "req", axis=0, tiled=True)
    n_in = 3 * heads_w + ff_w
    base = jnp.dot(full_ln, gathered[:, :n_in], preferred_element_type=jnp.float32)
    base_q = base[:, :heads_w]
    base_k = base[:, heads_w : 2 * heads_w]
    base_v = base[:, 2 * heads_w : 3 * heads_w]
    query = rotate(
        (base_q + lift(picked[0], up_query)).reshape(tok, heads_w // HS, HS), pos
    ).astype(jnp.bfloat16)
    keys = rotate(base_k.reshape(tok, heads_w // HS, HS), pos).astype(jnp.bfloat16)
    value = (
        (base_v + lift(picked[1], up_value)).astype(jnp.bfloat16).reshape(tok, heads_w // HS, HS)
    )
    scores = jnp.einsum("qhd,khd->hqk", query, keys, preferred_element_type=jnp.float32) * HS ** (
        -0.5
    )
    scores = jnp.where(mask[None, :, :], scores, -1e30)
    top = jnp.max(scores, axis=2, keepdims=True)
    weights = jnp.exp(scores - top)
    probs = (weights / jnp.sum(weights, axis=2, keepdims=True)).astype(jnp.bfloat16)
    mixed_heads = jnp.einsum("hqk,khd->qhd", probs, value, preferred_element_type=jnp.float32)
    attn = mixed_heads.astype(jnp.bfloat16).reshape(tok, heads_w)
    hidden_pre = base[:, 3 * heads_w :]
    hidden_pre = hidden_pre + lift(picked[2], up_fc) + b_fc_in
    hidden = gelu_tanh(hidden_pre).astype(jnp.bfloat16)
    part = lax.dot_general(
        attn,
        gathered[:, n_in:],
        (((1,), (1,)), ((), ())),
        preferred_element_type=jnp.float32,
    )
    part = part + jnp.einsum(
        "tf,rfc->trc", hidden, fo_rows, preferred_element_type=jnp.float32
    ).reshape(tok, groups * fo_rows.shape[2])
    shares = lax.psum_scatter(part, "mlp", scatter_dimension=1, tiled=True)
    result = (own_x.astype(jnp.float32) + shares + b_fc_out).astype(jnp.bfloat16)
    back_flat = result.reshape(pg_dev, page_len * width_m)
    leaving = jnp.dot(take.T, back_flat, preferred_element_type=jnp.float32).astype(jnp.bfloat16)
    leaving = leaving.reshape(groups, per_owner, page_len * width_m)
    returned = lax.all_to_all(leaving, "req", split_axis=0, concat_axis=0, tiled=True)
    pages_back = jnp.dot(
        place.T, returned.reshape(slots, page_len * width_m), preferred_element_type=jnp.float32
    )
    return pages_back.astype(jnp.bfloat16).reshape(pg_dev, page_len, width_m)


def solution(mesh):
    in_specs = (
        P("req", None, "mlp"),
        P("req"),
        P("req"),
        P("req"),
        P(),
        P(),
        P("req", "mlp"),
        P("req", "mlp"),
        P("req", "mlp"),
        P("mlp", "req"),
        P("mlp", None),
        P(None, "mlp"),
        P("mlp", None),
        P(None, "mlp"),
        P("req", "mlp"),
        P("mlp"),
        P("mlp", None),
        P(None, "mlp"),
        P("mlp", "req"),
        P("mlp"),
    )
    out_specs = P("req", None, "mlp")
    return jax.shard_map(
        on_device, mesh=mesh, in_specs=in_specs, out_specs=out_specs, check_vma=False
    )
```

```python
import jax
import jax.numpy as jnp
from jax import lax
from jax.sharding import PartitionSpec as P

HS = 256
ROT = 64
NAD = 64
R = 16


EPS = 1e-05


def gelu_tanh(v):
    return 0.5 * v * (1.0 + jnp.tanh(0.7978845608028654 * (v + 0.044715 * v * v * v)))


def rotate(block, pos):
    half = ROT // 2
    freq = jnp.power(10000.0, -jnp.arange(half).astype(jnp.float32) * 2.0 / ROT)
    angle = pos.astype(jnp.float32)[:, None, None] * freq[None, None, :]
    cosine = jnp.cos(angle)
    sine = jnp.sin(angle)
    even = block[:, :, 0:ROT:2]
    odd = block[:, :, 1:ROT:2]
    turned = jnp.stack([even * cosine - odd * sine, odd * cosine + even * sine], axis=-1)
    turned = turned.reshape(block.shape[0], block.shape[1], ROT)
    return jnp.concatenate([turned, block[:, :, ROT:]], axis=2)


def rotate_split(block, pos):
    half = ROT // 2
    freq = jnp.power(10000.0, -jnp.arange(half).astype(jnp.float32) * 2.0 / ROT)
    angle = pos.astype(jnp.float32)[:, None, None] * freq[None, None, :]
    cosine = jnp.cos(angle)
    sine = jnp.sin(angle)
    even = block[:, :, :half]
    odd = block[:, :, half:ROT]
    return jnp.concatenate(
        [even * cosine - odd * sine, odd * cosine + even * sine, block[:, :, ROT:]], axis=2
    )


def on_device(
    x_pages,
    page_owner,
    request_id,
    adapter_table,
    ln_gain,
    ln_bias,
    w_query,
    w_key,
    w_value,
    w_attn_out,
    down_query,
    up_query,
    down_value,
    up_value,
    w_fc_in,
    b_fc_in,
    down_fc,
    up_fc,
    w_fc_out,
    b_fc_out,
):
    groups = lax.axis_size("req")
    pg_dev = x_pages.shape[0]
    page_len = x_pages.shape[1]
    width_m = x_pages.shape[2]
    tok = request_id.shape[0]
    per_owner = pg_dev // groups + 1
    slots = groups * per_owner
    page_iota = jnp.arange(pg_dev)
    earlier = (page_owner[None, :] == page_owner[:, None]) & (
        page_iota[None, :] < page_iota[:, None]
    )
    rank = jnp.sum(earlier.astype(jnp.int32), axis=1)
    slot = page_owner * per_owner + rank
    place = (slot[None, :] == jnp.arange(slots)[:, None]).astype(jnp.bfloat16)
    flat_pages = x_pages.reshape(pg_dev, page_len * width_m)
    outgoing = jnp.dot(place, flat_pages, preferred_element_type=jnp.float32).astype(jnp.bfloat16)
    outgoing = outgoing.reshape(groups, per_owner, page_len * width_m)
    filled = jnp.sum(place, axis=1).reshape(groups, per_owner)
    arrived, marks = (
        lax.all_to_all(outgoing, "req", split_axis=0, concat_axis=0, tiled=True),
        lax.all_to_all(filled, "req", split_axis=0, concat_axis=0, tiled=True),
    )
    valid = marks.reshape(slots).astype(jnp.float32)
    position = jnp.cumsum(valid) - 1.0
    take = (
        (position[None, :] == jnp.arange(pg_dev).astype(jnp.float32)[:, None])
        & (valid[None, :] > 0.5)
    ).astype(jnp.bfloat16)
    own_x = jnp.dot(
        take, arrived.reshape(slots, page_len * width_m), preferred_element_type=jnp.float32
    )
    own_x = own_x.astype(jnp.bfloat16).reshape(tok, width_m)
    column = lax.axis_index("mlp") * width_m
    n_mlp = lax.axis_size("mlp")
    copies = jnp.broadcast_to(own_x[None], (n_mlp, tok, width_m))
    spread_x = lax.all_to_all(copies, "mlp", split_axis=0, concat_axis=0, tiled=True)
    whole = jnp.transpose(spread_x, (1, 0, 2)).reshape(tok, n_mlp * width_m).astype(jnp.float32)
    mean = jnp.mean(whole, axis=1, keepdims=True)
    var = jnp.mean(jnp.square(whole - mean), axis=1, keepdims=True)
    full_ln = ((whole - mean) * lax.rsqrt(var + EPS) * ln_gain + ln_bias).astype(jnp.bfloat16)
    ln_m = lax.dynamic_slice_in_dim(full_ln, column, width_m, 1)
    local_req = request_id - lax.axis_index("req") * tok
    lookup = local_req[:, None] == jnp.arange(tok)[None, :]
    adapter = jnp.sum(jnp.where(lookup, adapter_table[None, :], 0), axis=1)
    onehot = (adapter[:, None] == jnp.arange(NAD)[None, :]).astype(jnp.float32)
    onehot_low = onehot.astype(jnp.bfloat16)

    def pick(down):
        spread = jnp.dot(ln_m, down, preferred_element_type=jnp.float32).reshape(tok, NAD, R)
        return jnp.sum(spread * onehot[:, :, None], axis=1)

    picked = lax.psum((pick(down_query), pick(down_value), pick(down_fc)), "mlp")

    def lift(chosen, up):
        expanded = (onehot_low[:, :, None] * chosen.astype(jnp.bfloat16)[:, None, :]).reshape(
            tok, NAD * R
        )
        return jnp.dot(expanded, up, preferred_element_type=jnp.float32)

    row_iota = jnp.arange(tok)
    start = jnp.sum((request_id[None, :] < request_id[:, None]).astype(jnp.int32), axis=1)
    pos = row_iota - start
    mask = (request_id[:, None] == request_id[None, :]) & (row_iota[None, :] <= row_iota[:, None])
    heads_w = w_query.shape[1]
    ff_w = w_fc_in.shape[1]
    def pair_major(w):
        rows = w.shape[0]
        lead = w[:, :ROT].reshape(rows, ROT // 2, 2).transpose(0, 2, 1).reshape(rows, ROT)
        return jnp.concatenate([lead, w[:, ROT:]], axis=1)

    packed = jnp.concatenate(
        [pair_major(w_query), pair_major(w_key), w_value, w_fc_in, w_attn_out.T, w_fc_out.T],
        axis=1,
    )
    gathered = lax.all_gather(packed, "req", axis=0, tiled=True)
    n_in = 3 * heads_w + ff_w
    base = jnp.dot(full_ln, gathered[:, :n_in], preferred_element_type=jnp.float32)
    base_q = base[:, :heads_w]
    base_k = base[:, heads_w : 2 * heads_w]
    base_v = base[:, 2 * heads_w : 3 * heads_w]
    query = rotate_split(
        (base_q + lift(picked[0], pair_major(up_query))).reshape(tok, heads_w // HS, HS), pos
    ).astype(jnp.bfloat16)
    keys = rotate_split(base_k.reshape(tok, heads_w // HS, HS), pos).astype(jnp.bfloat16)
    value = (
        (base_v + lift(picked[1], up_value)).astype(jnp.bfloat16).reshape(tok, heads_w // HS, HS)
    )
    scores = jnp.einsum("qhd,khd->hqk", query, keys, preferred_element_type=jnp.float32) * HS ** (
        -0.5
    )
    scores = jnp.where(mask[None, :, :], scores, -1e30)
    top = jnp.max(scores, axis=2, keepdims=True)
    weights = jnp.exp(scores - top)
    probs = (weights / jnp.sum(weights, axis=2, keepdims=True)).astype(jnp.bfloat16)
    mixed_heads = jnp.einsum("hqk,khd->qhd", probs, value, preferred_element_type=jnp.float32)
    attn = mixed_heads.astype(jnp.bfloat16).reshape(tok, heads_w)
    hidden_pre = base[:, 3 * heads_w :]
    hidden_pre = hidden_pre + lift(picked[2], up_fc) + b_fc_in
    hidden = gelu_tanh(hidden_pre).astype(jnp.bfloat16)
    joined = jnp.concatenate([attn, hidden], axis=1)
    part = lax.dot_general(
        joined,
        gathered[:, n_in:],
        (((1,), (1,)), ((), ())),
        preferred_element_type=jnp.float32,
    )
    shares = lax.psum_scatter(
        part.astype(jnp.bfloat16), "mlp", scatter_dimension=1, tiled=True
    ).astype(jnp.float32)
    result = (own_x.astype(jnp.float32) + shares + b_fc_out).astype(jnp.bfloat16)
    back_flat = result.reshape(pg_dev, page_len * width_m)
    leaving = jnp.dot(take.T, back_flat, preferred_element_type=jnp.float32).astype(jnp.bfloat16)
    leaving = leaving.reshape(groups, per_owner, page_len * width_m)
    returned = lax.all_to_all(leaving, "req", split_axis=0, concat_axis=0, tiled=True)
    pages_back = jnp.dot(
        place.T, returned.reshape(slots, page_len * width_m), preferred_element_type=jnp.float32
    )
    return pages_back.astype(jnp.bfloat16).reshape(pg_dev, page_len, width_m)


def solution(mesh):
    in_specs = (
        P("req", None, "mlp"),
        P("req"),
        P("req"),
        P("req"),
        P(),
        P(),
        P("req", "mlp"),
        P("req", "mlp"),
        P("req", "mlp"),
        P("mlp", "req"),
        P("mlp", None),
        P(None, "mlp"),
        P("mlp", None),
        P(None, "mlp"),
        P("req", "mlp"),
        P("mlp"),
        P("mlp", None),
        P(None, "mlp"),
        P("mlp", "req"),
        P("mlp"),
    )
    out_specs = P("req", None, "mlp")
    return jax.shard_map(
        on_device, mesh=mesh, in_specs=in_specs, out_specs=out_specs, check_vma=False
    )
```

```python
import jax
import jax.numpy as jnp
from jax import lax
from jax.sharding import PartitionSpec as P

HS = 256
ROT = 64
NAD = 64
R = 16


EPS = 1e-05


def gelu_tanh(v):
    return 0.5 * v * (1.0 + jnp.tanh(0.7978845608028654 * (v + 0.044715 * v * v * v)))


def rotate(block, pos):
    half = ROT // 2
    freq = jnp.power(10000.0, -jnp.arange(half).astype(jnp.float32) * 2.0 / ROT)
    angle = pos.astype(jnp.float32)[:, None, None] * freq[None, None, :]
    cosine = jnp.cos(angle)
    sine = jnp.sin(angle)
    even = block[:, :, 0:ROT:2]
    odd = block[:, :, 1:ROT:2]
    turned = jnp.stack([even * cosine - odd * sine, odd * cosine + even * sine], axis=-1)
    turned = turned.reshape(block.shape[0], block.shape[1], ROT)
    return jnp.concatenate([turned, block[:, :, ROT:]], axis=2)


def rotate_split(block, pos):
    half = ROT // 2
    freq = jnp.power(10000.0, -jnp.arange(half).astype(jnp.float32) * 2.0 / ROT)
    angle = pos.astype(jnp.float32)[:, None, None] * freq[None, None, :]
    cosine = jnp.cos(angle)
    sine = jnp.sin(angle)
    even = block[:, :, :half]
    odd = block[:, :, half:ROT]
    return jnp.concatenate(
        [even * cosine - odd * sine, odd * cosine + even * sine, block[:, :, ROT:]], axis=2
    )


def on_device(
    x_pages,
    page_owner,
    request_id,
    adapter_table,
    ln_gain,
    ln_bias,
    w_query,
    w_key,
    w_value,
    w_attn_out,
    down_query,
    up_query,
    down_value,
    up_value,
    w_fc_in,
    b_fc_in,
    down_fc,
    up_fc,
    w_fc_out,
    b_fc_out,
):
    groups = lax.axis_size("req")
    pg_dev = x_pages.shape[0]
    page_len = x_pages.shape[1]
    width_m = x_pages.shape[2]
    tok = request_id.shape[0]
    per_owner = pg_dev // groups + 1
    slots = groups * per_owner
    page_iota = jnp.arange(pg_dev)
    earlier = (page_owner[None, :] == page_owner[:, None]) & (
        page_iota[None, :] < page_iota[:, None]
    )
    rank = jnp.sum(earlier.astype(jnp.int32), axis=1)
    slot = page_owner * per_owner + rank
    place = (slot[None, :] == jnp.arange(slots)[:, None]).astype(jnp.bfloat16)
    flat_pages = x_pages.reshape(pg_dev, page_len * width_m)
    outgoing = jnp.dot(place, flat_pages, preferred_element_type=jnp.float32).astype(jnp.bfloat16)
    outgoing = outgoing.reshape(groups, per_owner, page_len * width_m)
    filled = jnp.sum(place, axis=1).reshape(groups, per_owner)
    arrived, marks = (
        lax.all_to_all(outgoing, "req", split_axis=0, concat_axis=0, tiled=True),
        lax.all_to_all(filled, "req", split_axis=0, concat_axis=0, tiled=True),
    )
    valid = marks.reshape(slots).astype(jnp.float32)
    position = jnp.cumsum(valid) - 1.0
    take = (
        (position[None, :] == jnp.arange(pg_dev).astype(jnp.float32)[:, None])
        & (valid[None, :] > 0.5)
    ).astype(jnp.bfloat16)
    own_x = jnp.dot(
        take, arrived.reshape(slots, page_len * width_m), preferred_element_type=jnp.float32
    )
    own_x = own_x.astype(jnp.bfloat16).reshape(tok, width_m)
    column = lax.axis_index("mlp") * width_m
    n_mlp = lax.axis_size("mlp")
    copies = jnp.broadcast_to(own_x[None], (n_mlp, tok, width_m))
    spread_x = lax.all_to_all(copies, "mlp", split_axis=0, concat_axis=0, tiled=True)
    whole = jnp.transpose(spread_x, (1, 0, 2)).reshape(tok, n_mlp * width_m).astype(jnp.float32)
    mean = jnp.mean(whole, axis=1, keepdims=True)
    var = jnp.mean(jnp.square(whole - mean), axis=1, keepdims=True)
    full_ln = ((whole - mean) * lax.rsqrt(var + EPS) * ln_gain + ln_bias).astype(jnp.bfloat16)
    ln_m = lax.dynamic_slice_in_dim(full_ln, column, width_m, 1)
    local_req = request_id - lax.axis_index("req") * tok
    lookup = local_req[:, None] == jnp.arange(tok)[None, :]
    adapter = jnp.sum(jnp.where(lookup, adapter_table[None, :], 0), axis=1)
    onehot = (adapter[:, None] == jnp.arange(NAD)[None, :]).astype(jnp.float32)
    onehot_low = onehot.astype(jnp.bfloat16)

    def pick(down):
        spread = jnp.dot(ln_m, down, preferred_element_type=jnp.float32).reshape(tok, NAD, R)
        return jnp.sum(spread * onehot[:, :, None], axis=1)

    picked = lax.psum((pick(down_query), pick(down_value), pick(down_fc)), "mlp")

    def lift(chosen, up):
        expanded = (onehot_low[:, :, None] * chosen.astype(jnp.bfloat16)[:, None, :]).reshape(
            tok, NAD * R
        )
        return jnp.dot(expanded, up, preferred_element_type=jnp.float32)

    row_iota = jnp.arange(tok)
    start = jnp.sum((request_id[None, :] < request_id[:, None]).astype(jnp.int32), axis=1)
    pos = row_iota - start
    mask = (request_id[:, None] == request_id[None, :]) & (row_iota[None, :] <= row_iota[:, None])
    heads_w = w_query.shape[1]
    ff_w = w_fc_in.shape[1]
    def pair_major(w):
        rows = w.shape[0]
        lead = w[:, :ROT].reshape(rows, ROT // 2, 2).transpose(0, 2, 1).reshape(rows, ROT)
        return jnp.concatenate([lead, w[:, ROT:]], axis=1)

    packed = jnp.concatenate(
        [pair_major(w_query), pair_major(w_key), w_value, w_fc_in, w_attn_out.T, w_fc_out.T],
        axis=1,
    )
    gathered = lax.all_gather(packed, "req", axis=0, tiled=True)
    n_in = 3 * heads_w + ff_w
    base = jnp.dot(full_ln, gathered[:, :n_in], preferred_element_type=jnp.float32)
    base_q = base[:, :heads_w]
    base_k = base[:, heads_w : 2 * heads_w]
    base_v = base[:, 2 * heads_w : 3 * heads_w]
    query = rotate_split(
        (base_q + lift(picked[0], pair_major(up_query))).reshape(tok, heads_w // HS, HS), pos
    ).astype(jnp.bfloat16)
    keys = rotate_split(base_k.reshape(tok, heads_w // HS, HS), pos).astype(jnp.bfloat16)
    value = (
        (base_v + lift(picked[1], up_value)).astype(jnp.bfloat16).reshape(tok, heads_w // HS, HS)
    )
    scores = jnp.einsum("qhd,khd->hqk", query, keys, preferred_element_type=jnp.float32) * HS ** (
        -0.5
    )
    scores = jnp.where(mask[None, :, :], scores, -1e30)
    top = jnp.max(scores, axis=2, keepdims=True)
    weights = jnp.exp(scores - top)
    probs = (weights / jnp.sum(weights, axis=2, keepdims=True)).astype(jnp.bfloat16)
    mixed_heads = jnp.einsum("hqk,khd->qhd", probs, value, preferred_element_type=jnp.float32)
    attn = mixed_heads.astype(jnp.bfloat16).reshape(tok, heads_w)
    hidden_pre = base[:, 3 * heads_w :]
    hidden_pre = hidden_pre + lift(picked[2], up_fc) + b_fc_in
    hidden = gelu_tanh(hidden_pre).astype(jnp.bfloat16)
    joined = jnp.concatenate([attn, hidden], axis=1)
    part = lax.dot_general(
        joined,
        gathered[:, n_in:],
        (((1,), (1,)), ((), ())),
        preferred_element_type=jnp.float32,
    )
    shares = lax.psum_scatter(part, "mlp", scatter_dimension=1, tiled=True)
    result = (own_x.astype(jnp.float32) + shares + b_fc_out).astype(jnp.bfloat16)
    back_flat = result.reshape(pg_dev, page_len * width_m)
    leaving = jnp.dot(take.T, back_flat, preferred_element_type=jnp.float32).astype(jnp.bfloat16)
    leaving = leaving.reshape(groups, per_owner, page_len * width_m)
    returned = lax.all_to_all(leaving, "req", split_axis=0, concat_axis=0, tiled=True)
    pages_back = jnp.dot(
        place.T, returned.reshape(slots, page_len * width_m), preferred_element_type=jnp.float32
    )
    return pages_back.astype(jnp.bfloat16).reshape(pg_dev, page_len, width_m)


def solution(mesh):
    in_specs = (
        P("req", None, "mlp"),
        P("req"),
        P("req"),
        P("req"),
        P(),
        P(),
        P("req", "mlp"),
        P("req", "mlp"),
        P("req", "mlp"),
        P("mlp", "req"),
        P("mlp", None),
        P(None, "mlp"),
        P("mlp", None),
        P(None, "mlp"),
        P("req", "mlp"),
        P("mlp"),
        P("mlp", None),
        P(None, "mlp"),
        P("mlp", "req"),
        P("mlp"),
    )
    out_specs = P("req", None, "mlp")
    return jax.shard_map(
        on_device, mesh=mesh, in_specs=in_specs, out_specs=out_specs, check_vma=False
    )
```

```python
import jax
import jax.numpy as jnp
from jax import lax
from jax.experimental import pallas as pl
from jax.experimental.pallas import tpu as pltpu
from jax.sharding import PartitionSpec as P

HS = 256
ROT = 64
NAD = 64
R = 16


EPS = 1e-05


def gelu_tanh(v):
    return 0.5 * v * (1.0 + jnp.tanh(0.7978845608028654 * (v + 0.044715 * v * v * v)))


def rotate(block, pos):
    half = ROT // 2
    freq = jnp.power(10000.0, -jnp.arange(half).astype(jnp.float32) * 2.0 / ROT)
    angle = pos.astype(jnp.float32)[:, None, None] * freq[None, None, :]
    cosine = jnp.cos(angle)
    sine = jnp.sin(angle)
    even = block[:, :, 0:ROT:2]
    odd = block[:, :, 1:ROT:2]
    turned = jnp.stack([even * cosine - odd * sine, odd * cosine + even * sine], axis=-1)
    turned = turned.reshape(block.shape[0], block.shape[1], ROT)
    return jnp.concatenate([turned, block[:, :, ROT:]], axis=2)


def rotate_split(block, pos):
    half = ROT // 2
    freq = jnp.power(10000.0, -jnp.arange(half).astype(jnp.float32) * 2.0 / ROT)
    angle = pos.astype(jnp.float32)[:, None, None] * freq[None, None, :]
    cosine = jnp.cos(angle)
    sine = jnp.sin(angle)
    even = block[:, :, :half]
    odd = block[:, :, half:ROT]
    return jnp.concatenate(
        [even * cosine - odd * sine, odd * cosine + even * sine, block[:, :, ROT:]], axis=2
    )


def pack_kernel(wq_ref, wk_ref, wv_ref, wfi_ref, wao_ref, wfo_ref, out_ref):
    hw = wq_ref.shape[1]
    ff = wfi_ref.shape[1]
    rows = wq_ref.shape[0]
    src = lax.broadcasted_iota(jnp.int32, (hw, hw), 0)
    dst = lax.broadcasted_iota(jnp.int32, (hw, hw), 1)
    half = ROT // 2
    origin = jnp.where(
        dst < half, 2 * dst, jnp.where(dst < ROT, 2 * (dst - half) + 1, dst)
    )
    perm = (src == origin).astype(jnp.bfloat16)
    ident = (
        lax.broadcasted_iota(jnp.int32, (rows, rows), 0)
        == lax.broadcasted_iota(jnp.int32, (rows, rows), 1)
    ).astype(jnp.bfloat16)
    nt = (((1,), (1,)), ((), ()))
    out_ref[:, 0:hw] = jnp.dot(
        wq_ref[...], perm, preferred_element_type=jnp.float32
    ).astype(out_ref.dtype)
    out_ref[:, hw : 2 * hw] = jnp.dot(
        wk_ref[...], perm, preferred_element_type=jnp.float32
    ).astype(out_ref.dtype)
    out_ref[:, 2 * hw : 3 * hw] = wv_ref[...]
    out_ref[:, 3 * hw : 3 * hw + ff] = wfi_ref[...]
    base = 3 * hw + ff
    n_ao = wao_ref.shape[0]
    out_ref[:, base : base + n_ao] = lax.dot_general(
        ident, wao_ref[...], nt, preferred_element_type=jnp.float32
    ).astype(out_ref.dtype)
    n_fo = wfo_ref.shape[0]
    out_ref[:, base + n_ao : base + n_ao + n_fo] = lax.dot_general(
        ident, wfo_ref[...], nt, preferred_element_type=jnp.float32
    ).astype(out_ref.dtype)


def pack_weights(wq, wk, wv, wfi, wao, wfo):
    rows = wq.shape[0]
    cols = 3 * wq.shape[1] + wfi.shape[1] + wao.shape[0] + wfo.shape[0]
    vmem = pl.BlockSpec(memory_space=pltpu.VMEM)
    return pl.pallas_call(
        pack_kernel,
        out_shape=jax.ShapeDtypeStruct((rows, cols), wq.dtype),
        in_specs=[vmem] * 6,
        out_specs=vmem,
        cost_estimate=pl.CostEstimate(
            flops=2 * rows * (2 * wq.shape[1] ** 2 + rows * (wao.shape[0] + wfo.shape[0])),
            bytes_accessed=4 * rows * cols,
            transcendentals=0,
        ),
    )(wq, wk, wv, wfi, wao, wfo)


def on_device(
    x_pages,
    page_owner,
    request_id,
    adapter_table,
    ln_gain,
    ln_bias,
    w_query,
    w_key,
    w_value,
    w_attn_out,
    down_query,
    up_query,
    down_value,
    up_value,
    w_fc_in,
    b_fc_in,
    down_fc,
    up_fc,
    w_fc_out,
    b_fc_out,
):
    groups = lax.axis_size("req")
    pg_dev = x_pages.shape[0]
    page_len = x_pages.shape[1]
    width_m = x_pages.shape[2]
    tok = request_id.shape[0]
    per_owner = pg_dev // groups + 1
    slots = groups * per_owner
    page_iota = jnp.arange(pg_dev)
    earlier = (page_owner[None, :] == page_owner[:, None]) & (
        page_iota[None, :] < page_iota[:, None]
    )
    rank = jnp.sum(earlier.astype(jnp.int32), axis=1)
    slot = page_owner * per_owner + rank
    place = (slot[None, :] == jnp.arange(slots)[:, None]).astype(jnp.bfloat16)
    flat_pages = x_pages.reshape(pg_dev, page_len * width_m)
    outgoing = jnp.dot(place, flat_pages, preferred_element_type=jnp.float32).astype(jnp.bfloat16)
    outgoing = outgoing.reshape(groups, per_owner, page_len * width_m)
    filled = jnp.sum(place, axis=1).reshape(groups, per_owner)
    arrived, marks = (
        lax.all_to_all(outgoing, "req", split_axis=0, concat_axis=0, tiled=True),
        lax.all_to_all(filled, "req", split_axis=0, concat_axis=0, tiled=True),
    )
    valid = marks.reshape(slots).astype(jnp.float32)
    position = jnp.cumsum(valid) - 1.0
    take = (
        (position[None, :] == jnp.arange(pg_dev).astype(jnp.float32)[:, None])
        & (valid[None, :] > 0.5)
    ).astype(jnp.bfloat16)
    own_x = jnp.dot(
        take, arrived.reshape(slots, page_len * width_m), preferred_element_type=jnp.float32
    )
    own_x = own_x.astype(jnp.bfloat16).reshape(tok, width_m)
    column = lax.axis_index("mlp") * width_m
    n_mlp = lax.axis_size("mlp")
    copies = jnp.broadcast_to(own_x[None], (n_mlp, tok, width_m))
    spread_x = lax.all_to_all(copies, "mlp", split_axis=0, concat_axis=0, tiled=True)
    whole = jnp.transpose(spread_x, (1, 0, 2)).reshape(tok, n_mlp * width_m).astype(jnp.float32)
    mean = jnp.mean(whole, axis=1, keepdims=True)
    var = jnp.mean(jnp.square(whole - mean), axis=1, keepdims=True)
    full_ln = ((whole - mean) * lax.rsqrt(var + EPS) * ln_gain + ln_bias).astype(jnp.bfloat16)
    ln_m = lax.dynamic_slice_in_dim(full_ln, column, width_m, 1)
    local_req = request_id - lax.axis_index("req") * tok
    lookup = local_req[:, None] == jnp.arange(tok)[None, :]
    adapter = jnp.sum(jnp.where(lookup, adapter_table[None, :], 0), axis=1)
    onehot = (adapter[:, None] == jnp.arange(NAD)[None, :]).astype(jnp.float32)
    onehot_low = onehot.astype(jnp.bfloat16)

    def pick(down):
        spread = jnp.dot(ln_m, down, preferred_element_type=jnp.float32).reshape(tok, NAD, R)
        return jnp.sum(spread * onehot[:, :, None], axis=1)

    picked = lax.psum((pick(down_query), pick(down_value), pick(down_fc)), "mlp")

    def lift(chosen, up):
        expanded = (onehot_low[:, :, None] * chosen.astype(jnp.bfloat16)[:, None, :]).reshape(
            tok, NAD * R
        )
        return jnp.dot(expanded, up, preferred_element_type=jnp.float32)

    row_iota = jnp.arange(tok)
    start = jnp.sum((request_id[None, :] < request_id[:, None]).astype(jnp.int32), axis=1)
    pos = row_iota - start
    mask = (request_id[:, None] == request_id[None, :]) & (row_iota[None, :] <= row_iota[:, None])
    heads_w = w_query.shape[1]
    ff_w = w_fc_in.shape[1]
    def pair_major(w):
        rows = w.shape[0]
        lead = w[:, :ROT].reshape(rows, ROT // 2, 2).transpose(0, 2, 1).reshape(rows, ROT)
        return jnp.concatenate([lead, w[:, ROT:]], axis=1)

    packed = pack_weights(w_query, w_key, w_value, w_fc_in, w_attn_out, w_fc_out)
    gathered = lax.all_gather(packed, "req", axis=0, tiled=True)
    n_in = 3 * heads_w + ff_w
    base = jnp.dot(full_ln, gathered[:, :n_in], preferred_element_type=jnp.float32)
    base_q = base[:, :heads_w]
    base_k = base[:, heads_w : 2 * heads_w]
    base_v = base[:, 2 * heads_w : 3 * heads_w]
    query = rotate_split(
        (base_q + lift(picked[0], pair_major(up_query))).reshape(tok, heads_w // HS, HS), pos
    ).astype(jnp.bfloat16)
    keys = rotate_split(base_k.reshape(tok, heads_w // HS, HS), pos).astype(jnp.bfloat16)
    value = (
        (base_v + lift(picked[1], up_value)).astype(jnp.bfloat16).reshape(tok, heads_w // HS, HS)
    )
    scores = jnp.einsum("qhd,khd->hqk", query, keys, preferred_element_type=jnp.float32) * HS ** (
        -0.5
    )
    scores = jnp.where(mask[None, :, :], scores, -1e30)
    top = jnp.max(scores, axis=2, keepdims=True)
    weights = jnp.exp(scores - top)
    probs = (weights / jnp.sum(weights, axis=2, keepdims=True)).astype(jnp.bfloat16)
    mixed_heads = jnp.einsum("hqk,khd->qhd", probs, value, preferred_element_type=jnp.float32)
    attn = mixed_heads.astype(jnp.bfloat16).reshape(tok, heads_w)
    hidden_pre = base[:, 3 * heads_w :]
    hidden_pre = hidden_pre + lift(picked[2], up_fc) + b_fc_in
    hidden = gelu_tanh(hidden_pre).astype(jnp.bfloat16)
    joined = jnp.concatenate([attn, hidden], axis=1)
    part = lax.dot_general(
        joined,
        gathered[:, n_in:],
        (((1,), (1,)), ((), ())),
        preferred_element_type=jnp.float32,
    )
    shares = lax.psum_scatter(part, "mlp", scatter_dimension=1, tiled=True)
    result = (own_x.astype(jnp.float32) + shares + b_fc_out).astype(jnp.bfloat16)
    back_flat = result.reshape(pg_dev, page_len * width_m)
    leaving = jnp.dot(take.T, back_flat, preferred_element_type=jnp.float32).astype(jnp.bfloat16)
    leaving = leaving.reshape(groups, per_owner, page_len * width_m)
    returned = lax.all_to_all(leaving, "req", split_axis=0, concat_axis=0, tiled=True)
    pages_back = jnp.dot(
        place.T, returned.reshape(slots, page_len * width_m), preferred_element_type=jnp.float32
    )
    return pages_back.astype(jnp.bfloat16).reshape(pg_dev, page_len, width_m)


def solution(mesh):
    in_specs = (
        P("req", None, "mlp"),
        P("req"),
        P("req"),
        P("req"),
        P(),
        P(),
        P("req", "mlp"),
        P("req", "mlp"),
        P("req", "mlp"),
        P("mlp", "req"),
        P("mlp", None),
        P(None, "mlp"),
        P("mlp", None),
        P(None, "mlp"),
        P("req", "mlp"),
        P("mlp"),
        P("mlp", None),
        P(None, "mlp"),
        P("mlp", "req"),
        P("mlp"),
    )
    out_specs = P("req", None, "mlp")
    return jax.shard_map(
        on_device, mesh=mesh, in_specs=in_specs, out_specs=out_specs, check_vma=False
    )
```

```python
import jax
import jax.numpy as jnp
from jax import lax
from jax.experimental import pallas as pl
from jax.experimental.pallas import tpu as pltpu
from jax.sharding import PartitionSpec as P

HS = 256
ROT = 64
NAD = 64
R = 16


EPS = 1e-05


def gelu_tanh(v):
    return 0.5 * v * (1.0 + jnp.tanh(0.7978845608028654 * (v + 0.044715 * v * v * v)))


def rotate(block, pos):
    half = ROT // 2
    freq = jnp.power(10000.0, -jnp.arange(half).astype(jnp.float32) * 2.0 / ROT)
    angle = pos.astype(jnp.float32)[:, None, None] * freq[None, None, :]
    cosine = jnp.cos(angle)
    sine = jnp.sin(angle)
    even = block[:, :, 0:ROT:2]
    odd = block[:, :, 1:ROT:2]
    turned = jnp.stack([even * cosine - odd * sine, odd * cosine + even * sine], axis=-1)
    turned = turned.reshape(block.shape[0], block.shape[1], ROT)
    return jnp.concatenate([turned, block[:, :, ROT:]], axis=2)


def rotate_split(block, pos):
    half = ROT // 2
    freq = jnp.power(10000.0, -jnp.arange(half).astype(jnp.float32) * 2.0 / ROT)
    angle = pos.astype(jnp.float32)[:, None, None] * freq[None, None, :]
    cosine = jnp.cos(angle)
    sine = jnp.sin(angle)
    even = block[:, :, :half]
    odd = block[:, :, half:ROT]
    return jnp.concatenate(
        [even * cosine - odd * sine, odd * cosine + even * sine, block[:, :, ROT:]], axis=2
    )


def pack_kernel(wq_ref, wk_ref, wv_ref, wfi_ref, wao_ref, wfo_ref, out_ref):
    hw = wq_ref.shape[1]
    ff = wfi_ref.shape[1]
    rows = wq_ref.shape[0]
    src = lax.broadcasted_iota(jnp.int32, (hw, hw), 0)
    dst = lax.broadcasted_iota(jnp.int32, (hw, hw), 1)
    half = ROT // 2
    origin = jnp.where(
        dst < half, 2 * dst, jnp.where(dst < ROT, 2 * (dst - half) + 1, dst)
    )
    perm = (src == origin).astype(jnp.bfloat16)
    ident = (
        lax.broadcasted_iota(jnp.int32, (rows, rows), 0)
        == lax.broadcasted_iota(jnp.int32, (rows, rows), 1)
    ).astype(jnp.bfloat16)
    nt = (((1,), (1,)), ((), ()))
    out_ref[:, 0:hw] = jnp.dot(
        wq_ref[...], perm, preferred_element_type=jnp.float32
    ).astype(out_ref.dtype)
    out_ref[:, hw : 2 * hw] = jnp.dot(
        wk_ref[...], perm, preferred_element_type=jnp.float32
    ).astype(out_ref.dtype)
    out_ref[:, 2 * hw : 3 * hw] = wv_ref[...]
    out_ref[:, 3 * hw : 3 * hw + ff] = wfi_ref[...]
    base = 3 * hw + ff
    n_ao = wao_ref.shape[0]
    out_ref[:, base : base + n_ao] = lax.dot_general(
        ident, wao_ref[...], nt, preferred_element_type=jnp.float32
    ).astype(out_ref.dtype)
    n_fo = wfo_ref.shape[0]
    out_ref[:, base + n_ao : base + n_ao + n_fo] = lax.dot_general(
        ident, wfo_ref[...], nt, preferred_element_type=jnp.float32
    ).astype(out_ref.dtype)


def pack_weights(wq, wk, wv, wfi, wao, wfo):
    rows = wq.shape[0]
    cols = 3 * wq.shape[1] + wfi.shape[1] + wao.shape[0] + wfo.shape[0]
    vmem = pl.BlockSpec(memory_space=pltpu.VMEM)
    return pl.pallas_call(
        pack_kernel,
        out_shape=jax.ShapeDtypeStruct((rows, cols), wq.dtype),
        in_specs=[vmem] * 6,
        out_specs=vmem,
        cost_estimate=pl.CostEstimate(
            flops=2 * rows * (2 * wq.shape[1] ** 2 + rows * (wao.shape[0] + wfo.shape[0])),
            bytes_accessed=4 * rows * cols,
            transcendentals=0,
        ),
    )(wq, wk, wv, wfi, wao, wfo)


RING_Z = 8


def ring_gather(block, n, step):
    right = {}
    left = {}
    cur_r = block
    cur_l = block
    for t in range(1, n // 2):
        cur_r = lax.ppermute(cur_r, "req", step(1))
        cur_l = lax.ppermute(cur_l, "req", step(-1))
        right[t] = cur_r
        left[t] = cur_l
    cut = block.shape[0] // 2
    far_a = lax.ppermute(cur_r[:cut], "req", step(1))
    far_b = lax.ppermute(cur_l[cut:], "req", step(-1))
    rel = [block]
    for k in range(1, n):
        if k < n // 2:
            rel.append(left[k])
        elif k == n // 2:
            rel.append(jnp.concatenate([far_a, far_b], axis=0))
        else:
            rel.append(right[n - k])
    return jnp.stack(rel, axis=0)


def on_device(
    x_pages,
    page_owner,
    request_id,
    adapter_table,
    ln_gain,
    ln_bias,
    w_query,
    w_key,
    w_value,
    w_attn_out,
    down_query,
    up_query,
    down_value,
    up_value,
    w_fc_in,
    b_fc_in,
    down_fc,
    up_fc,
    w_fc_out,
    b_fc_out,
):
    groups = lax.axis_size("req")
    pg_dev = x_pages.shape[0]
    page_len = x_pages.shape[1]
    width_m = x_pages.shape[2]
    tok = request_id.shape[0]
    per_owner = pg_dev // groups + 1
    slots = groups * per_owner
    page_iota = jnp.arange(pg_dev)
    earlier = (page_owner[None, :] == page_owner[:, None]) & (
        page_iota[None, :] < page_iota[:, None]
    )
    rank = jnp.sum(earlier.astype(jnp.int32), axis=1)
    slot = page_owner * per_owner + rank
    place = (slot[None, :] == jnp.arange(slots)[:, None]).astype(jnp.bfloat16)
    flat_pages = x_pages.reshape(pg_dev, page_len * width_m)
    outgoing = jnp.dot(place, flat_pages, preferred_element_type=jnp.float32).astype(jnp.bfloat16)
    outgoing = outgoing.reshape(groups, per_owner, page_len * width_m)
    filled = jnp.sum(place, axis=1).reshape(groups, per_owner)
    arrived, marks = (
        lax.all_to_all(outgoing, "req", split_axis=0, concat_axis=0, tiled=True),
        lax.all_to_all(filled, "req", split_axis=0, concat_axis=0, tiled=True),
    )
    valid = marks.reshape(slots).astype(jnp.float32)
    position = jnp.cumsum(valid) - 1.0
    take = (
        (position[None, :] == jnp.arange(pg_dev).astype(jnp.float32)[:, None])
        & (valid[None, :] > 0.5)
    ).astype(jnp.bfloat16)
    own_x = jnp.dot(
        take, arrived.reshape(slots, page_len * width_m), preferred_element_type=jnp.float32
    )
    own_x = own_x.astype(jnp.bfloat16).reshape(tok, width_m)
    column = lax.axis_index("mlp") * width_m
    n_mlp = lax.axis_size("mlp")
    copies = jnp.broadcast_to(own_x[None], (n_mlp, tok, width_m))
    spread_x = lax.all_to_all(copies, "mlp", split_axis=0, concat_axis=0, tiled=True)
    whole = jnp.transpose(spread_x, (1, 0, 2)).reshape(tok, n_mlp * width_m).astype(jnp.float32)
    mean = jnp.mean(whole, axis=1, keepdims=True)
    var = jnp.mean(jnp.square(whole - mean), axis=1, keepdims=True)
    full_ln = ((whole - mean) * lax.rsqrt(var + EPS) * ln_gain + ln_bias).astype(jnp.bfloat16)
    ln_m = lax.dynamic_slice_in_dim(full_ln, column, width_m, 1)
    local_req = request_id - lax.axis_index("req") * tok
    lookup = local_req[:, None] == jnp.arange(tok)[None, :]
    adapter = jnp.sum(jnp.where(lookup, adapter_table[None, :], 0), axis=1)
    onehot = (adapter[:, None] == jnp.arange(NAD)[None, :]).astype(jnp.float32)
    onehot_low = onehot.astype(jnp.bfloat16)

    def pick(down):
        spread = jnp.dot(ln_m, down, preferred_element_type=jnp.float32).reshape(tok, NAD, R)
        return jnp.sum(spread * onehot[:, :, None], axis=1)

    picked = lax.psum((pick(down_query), pick(down_value), pick(down_fc)), "mlp")

    def lift(chosen, up):
        expanded = (onehot_low[:, :, None] * chosen.astype(jnp.bfloat16)[:, None, :]).reshape(
            tok, NAD * R
        )
        return jnp.dot(expanded, up, preferred_element_type=jnp.float32)

    row_iota = jnp.arange(tok)
    start = jnp.sum((request_id[None, :] < request_id[:, None]).astype(jnp.int32), axis=1)
    pos = row_iota - start
    mask = (request_id[:, None] == request_id[None, :]) & (row_iota[None, :] <= row_iota[:, None])
    heads_w = w_query.shape[1]
    ff_w = w_fc_in.shape[1]
    def pair_major(w):
        rows = w.shape[0]
        lead = w[:, :ROT].reshape(rows, ROT // 2, 2).transpose(0, 2, 1).reshape(rows, ROT)
        return jnp.concatenate([lead, w[:, ROT:]], axis=1)

    packed = pack_weights(w_query, w_key, w_value, w_fc_in, w_attn_out, w_fc_out)
    n_in = 3 * heads_w + ff_w
    n_z = RING_Z
    n_x = groups // n_z
    me = lax.axis_index("req")
    my_x = me // n_z
    my_z = me % n_z
    z_step = lambda d: [(i, (i // n_z) * n_z + (i % n_z + d) % n_z) for i in range(groups)]
    x_step = lambda d: [(i, ((i // n_z + d) % n_x) * n_z + i % n_z) for i in range(groups)]
    half_a = ring_gather(ring_gather(packed[:, :n_in], n_z, z_step), n_x, x_step)
    half_b = ring_gather(ring_gather(packed[:, n_in:], n_x, x_step), n_z, z_step)
    rows_w = packed.shape[0]
    ln_grid = full_ln.reshape(tok, n_x, n_z, rows_w)
    ln_grid = jnp.roll(jnp.roll(ln_grid, -my_x, axis=1), -my_z, axis=2)
    base = jnp.dot(
        ln_grid.reshape(tok, groups * rows_w),
        half_a.reshape(groups * rows_w, n_in),
        preferred_element_type=jnp.float32,
    )
    base_q = base[:, :heads_w]
    base_k = base[:, heads_w : 2 * heads_w]
    base_v = base[:, 2 * heads_w : 3 * heads_w]
    query = rotate_split(
        (base_q + lift(picked[0], pair_major(up_query))).reshape(tok, heads_w // HS, HS), pos
    ).astype(jnp.bfloat16)
    keys = rotate_split(base_k.reshape(tok, heads_w // HS, HS), pos).astype(jnp.bfloat16)
    value = (
        (base_v + lift(picked[1], up_value)).astype(jnp.bfloat16).reshape(tok, heads_w // HS, HS)
    )
    scores = jnp.einsum("qhd,khd->hqk", query, keys, preferred_element_type=jnp.float32) * HS ** (
        -0.5
    )
    scores = jnp.where(mask[None, :, :], scores, -1e30)
    top = jnp.max(scores, axis=2, keepdims=True)
    weights = jnp.exp(scores - top)
    probs = (weights / jnp.sum(weights, axis=2, keepdims=True)).astype(jnp.bfloat16)
    mixed_heads = jnp.einsum("hqk,khd->qhd", probs, value, preferred_element_type=jnp.float32)
    attn = mixed_heads.astype(jnp.bfloat16).reshape(tok, heads_w)
    hidden_pre = base[:, 3 * heads_w :]
    hidden_pre = hidden_pre + lift(picked[2], up_fc) + b_fc_in
    hidden = gelu_tanh(hidden_pre).astype(jnp.bfloat16)
    joined = jnp.concatenate([attn, hidden], axis=1)
    part = lax.dot_general(
        joined,
        half_b.reshape(groups * rows_w, half_b.shape[-1]),
        (((1,), (1,)), ((), ())),
        preferred_element_type=jnp.float32,
    )
    part = part.reshape(tok, n_z, n_x, rows_w)
    part = jnp.roll(jnp.roll(part, my_z, axis=1), my_x, axis=2)
    part = jnp.transpose(part, (0, 2, 1, 3)).reshape(tok, groups * rows_w)
    shares = lax.psum_scatter(part, "mlp", scatter_dimension=1, tiled=True)
    result = (own_x.astype(jnp.float32) + shares + b_fc_out).astype(jnp.bfloat16)
    back_flat = result.reshape(pg_dev, page_len * width_m)
    leaving = jnp.dot(take.T, back_flat, preferred_element_type=jnp.float32).astype(jnp.bfloat16)
    leaving = leaving.reshape(groups, per_owner, page_len * width_m)
    returned = lax.all_to_all(leaving, "req", split_axis=0, concat_axis=0, tiled=True)
    pages_back = jnp.dot(
        place.T, returned.reshape(slots, page_len * width_m), preferred_element_type=jnp.float32
    )
    return pages_back.astype(jnp.bfloat16).reshape(pg_dev, page_len, width_m)


def solution(mesh):
    in_specs = (
        P("req", None, "mlp"),
        P("req"),
        P("req"),
        P("req"),
        P(),
        P(),
        P("req", "mlp"),
        P("req", "mlp"),
        P("req", "mlp"),
        P("mlp", "req"),
        P("mlp", None),
        P(None, "mlp"),
        P("mlp", None),
        P(None, "mlp"),
        P("req", "mlp"),
        P("mlp"),
        P("mlp", None),
        P(None, "mlp"),
        P("mlp", "req"),
        P("mlp"),
    )
    out_specs = P("req", None, "mlp")
    return jax.shard_map(
        on_device, mesh=mesh, in_specs=in_specs, out_specs=out_specs, check_vma=False
    )
```

```python
import jax
import jax.numpy as jnp
from jax import lax
from jax.experimental import pallas as pl
from jax.experimental.pallas import tpu as pltpu
from jax.sharding import PartitionSpec as P

HS = 256
ROT = 64
NAD = 64
R = 16


EPS = 1e-05


def gelu_tanh(v):
    return 0.5 * v * (1.0 + jnp.tanh(0.7978845608028654 * (v + 0.044715 * v * v * v)))


def rotate(block, pos):
    half = ROT // 2
    freq = jnp.power(10000.0, -jnp.arange(half).astype(jnp.float32) * 2.0 / ROT)
    angle = pos.astype(jnp.float32)[:, None, None] * freq[None, None, :]
    cosine = jnp.cos(angle)
    sine = jnp.sin(angle)
    even = block[:, :, 0:ROT:2]
    odd = block[:, :, 1:ROT:2]
    turned = jnp.stack([even * cosine - odd * sine, odd * cosine + even * sine], axis=-1)
    turned = turned.reshape(block.shape[0], block.shape[1], ROT)
    return jnp.concatenate([turned, block[:, :, ROT:]], axis=2)


def rotate_split(block, pos):
    half = ROT // 2
    freq = jnp.power(10000.0, -jnp.arange(half).astype(jnp.float32) * 2.0 / ROT)
    angle = pos.astype(jnp.float32)[:, None, None] * freq[None, None, :]
    cosine = jnp.cos(angle)
    sine = jnp.sin(angle)
    even = block[:, :, :half]
    odd = block[:, :, half:ROT]
    return jnp.concatenate(
        [even * cosine - odd * sine, odd * cosine + even * sine, block[:, :, ROT:]], axis=2
    )


def pack_kernel(wq_ref, wk_ref, wv_ref, wfi_ref, wao_ref, wfo_ref, out_ref):
    hw = wq_ref.shape[1]
    ff = wfi_ref.shape[1]
    rows = wq_ref.shape[0]
    src = lax.broadcasted_iota(jnp.int32, (hw, hw), 0)
    dst = lax.broadcasted_iota(jnp.int32, (hw, hw), 1)
    half = ROT // 2
    origin = jnp.where(
        dst < half, 2 * dst, jnp.where(dst < ROT, 2 * (dst - half) + 1, dst)
    )
    perm = (src == origin).astype(jnp.bfloat16)
    ident = (
        lax.broadcasted_iota(jnp.int32, (rows, rows), 0)
        == lax.broadcasted_iota(jnp.int32, (rows, rows), 1)
    ).astype(jnp.bfloat16)
    nt = (((1,), (1,)), ((), ()))
    out_ref[:, 0:hw] = jnp.dot(
        wq_ref[...], perm, preferred_element_type=jnp.float32
    ).astype(out_ref.dtype)
    out_ref[:, hw : 2 * hw] = jnp.dot(
        wk_ref[...], perm, preferred_element_type=jnp.float32
    ).astype(out_ref.dtype)
    out_ref[:, 2 * hw : 3 * hw] = wv_ref[...]
    out_ref[:, 3 * hw : 3 * hw + ff] = wfi_ref[...]
    base = 3 * hw + ff
    n_ao = wao_ref.shape[0]
    out_ref[:, base : base + n_ao] = lax.dot_general(
        ident, wao_ref[...], nt, preferred_element_type=jnp.float32
    ).astype(out_ref.dtype)
    n_fo = wfo_ref.shape[0]
    out_ref[:, base + n_ao : base + n_ao + n_fo] = lax.dot_general(
        ident, wfo_ref[...], nt, preferred_element_type=jnp.float32
    ).astype(out_ref.dtype)


def pack_weights(wq, wk, wv, wfi, wao, wfo):
    rows = wq.shape[0]
    cols = 3 * wq.shape[1] + wfi.shape[1] + wao.shape[0] + wfo.shape[0]
    vmem = pl.BlockSpec(memory_space=pltpu.VMEM)
    return pl.pallas_call(
        pack_kernel,
        out_shape=jax.ShapeDtypeStruct((rows, cols), wq.dtype),
        in_specs=[vmem] * 6,
        out_specs=vmem,
        cost_estimate=pl.CostEstimate(
            flops=2 * rows * (2 * wq.shape[1] ** 2 + rows * (wao.shape[0] + wfo.shape[0])),
            bytes_accessed=4 * rows * cols,
            transcendentals=0,
        ),
    )(wq, wk, wv, wfi, wao, wfo)


def on_device(
    x_pages,
    page_owner,
    request_id,
    adapter_table,
    ln_gain,
    ln_bias,
    w_query,
    w_key,
    w_value,
    w_attn_out,
    down_query,
    up_query,
    down_value,
    up_value,
    w_fc_in,
    b_fc_in,
    down_fc,
    up_fc,
    w_fc_out,
    b_fc_out,
):
    groups = lax.axis_size("req")
    pg_dev = x_pages.shape[0]
    page_len = x_pages.shape[1]
    width_m = x_pages.shape[2]
    tok = request_id.shape[0]
    per_owner = pg_dev // groups + 1
    slots = groups * per_owner
    page_iota = jnp.arange(pg_dev)
    earlier = (page_owner[None, :] == page_owner[:, None]) & (
        page_iota[None, :] < page_iota[:, None]
    )
    rank = jnp.sum(earlier.astype(jnp.int32), axis=1)
    slot = page_owner * per_owner + rank
    place = (slot[None, :] == jnp.arange(slots)[:, None]).astype(jnp.bfloat16)
    flat_pages = x_pages.reshape(pg_dev, page_len * width_m)
    outgoing = jnp.dot(place, flat_pages, preferred_element_type=jnp.float32).astype(jnp.bfloat16)
    outgoing = outgoing.reshape(groups, per_owner, page_len * width_m)
    filled = jnp.sum(place, axis=1).reshape(groups, per_owner)
    arrived, marks = (
        lax.all_to_all(outgoing, "req", split_axis=0, concat_axis=0, tiled=True),
        lax.all_to_all(filled, "req", split_axis=0, concat_axis=0, tiled=True),
    )
    valid = marks.reshape(slots).astype(jnp.float32)
    position = jnp.cumsum(valid) - 1.0
    take = (
        (position[None, :] == jnp.arange(pg_dev).astype(jnp.float32)[:, None])
        & (valid[None, :] > 0.5)
    ).astype(jnp.bfloat16)
    own_x = jnp.dot(
        take, arrived.reshape(slots, page_len * width_m), preferred_element_type=jnp.float32
    )
    own_x = own_x.astype(jnp.bfloat16).reshape(tok, width_m)
    column = lax.axis_index("mlp") * width_m
    n_mlp = lax.axis_size("mlp")
    copies = jnp.broadcast_to(own_x[None], (n_mlp, tok, width_m))
    spread_x = lax.all_to_all(copies, "mlp", split_axis=0, concat_axis=0, tiled=True)
    whole = jnp.transpose(spread_x, (1, 0, 2)).reshape(tok, n_mlp * width_m).astype(jnp.float32)
    mean = jnp.mean(whole, axis=1, keepdims=True)
    var = jnp.mean(jnp.square(whole - mean), axis=1, keepdims=True)
    full_ln = ((whole - mean) * lax.rsqrt(var + EPS) * ln_gain + ln_bias).astype(jnp.bfloat16)
    ln_m = lax.dynamic_slice_in_dim(full_ln, column, width_m, 1)
    local_req = request_id - lax.axis_index("req") * tok
    lookup = local_req[:, None] == jnp.arange(tok)[None, :]
    adapter = jnp.sum(jnp.where(lookup, adapter_table[None, :], 0), axis=1)
    onehot = (adapter[:, None] == jnp.arange(NAD)[None, :]).astype(jnp.float32)
    onehot_low = onehot.astype(jnp.bfloat16)

    def pick(down):
        spread = jnp.dot(ln_m, down, preferred_element_type=jnp.float32).reshape(tok, NAD, R)
        return jnp.sum(spread * onehot[:, :, None], axis=1)

    picked = lax.psum((pick(down_query), pick(down_value), pick(down_fc)), "mlp")

    def lift(chosen, up):
        expanded = (onehot_low[:, :, None] * chosen.astype(jnp.bfloat16)[:, None, :]).reshape(
            tok, NAD * R
        )
        return jnp.dot(expanded, up, preferred_element_type=jnp.float32)

    row_iota = jnp.arange(tok)
    start = jnp.sum((request_id[None, :] < request_id[:, None]).astype(jnp.int32), axis=1)
    pos = row_iota - start
    mask = (request_id[:, None] == request_id[None, :]) & (row_iota[None, :] <= row_iota[:, None])
    heads_w = w_query.shape[1]
    ff_w = w_fc_in.shape[1]
    def pair_major(w):
        rows = w.shape[0]
        lead = w[:, :ROT].reshape(rows, ROT // 2, 2).transpose(0, 2, 1).reshape(rows, ROT)
        return jnp.concatenate([lead, w[:, ROT:]], axis=1)

    packed = pack_weights(w_query, w_key, w_value, w_fc_in, w_attn_out, w_fc_out)
    gathered = lax.all_gather(packed, "req", axis=0, tiled=True)
    n_in = 3 * heads_w + ff_w
    base = jnp.dot(full_ln, gathered[:, :n_in], preferred_element_type=jnp.float32)
    base_q = base[:, :heads_w]
    base_k = base[:, heads_w : 2 * heads_w]
    base_v = base[:, 2 * heads_w : 3 * heads_w]
    query = rotate_split(
        (base_q + lift(picked[0], pair_major(up_query))).reshape(tok, heads_w // HS, HS), pos
    ).astype(jnp.bfloat16)
    keys = rotate_split(base_k.reshape(tok, heads_w // HS, HS), pos).astype(jnp.bfloat16)
    value = (
        (base_v + lift(picked[1], up_value)).astype(jnp.bfloat16).reshape(tok, heads_w // HS, HS)
    )
    scores = jnp.einsum("qhd,khd->hqk", query, keys, preferred_element_type=jnp.float32) * HS ** (
        -0.5
    )
    scores = jnp.where(mask[None, :, :], scores, -1e30)
    top = jnp.max(scores, axis=2, keepdims=True)
    weights = jnp.exp(scores - top)
    probs = (weights / jnp.sum(weights, axis=2, keepdims=True)).astype(jnp.bfloat16)
    mixed_heads = jnp.einsum("hqk,khd->qhd", probs, value, preferred_element_type=jnp.float32)
    attn = mixed_heads.astype(jnp.bfloat16).reshape(tok, heads_w)
    hidden_pre = base[:, 3 * heads_w :]
    hidden_pre = hidden_pre + lift(picked[2], up_fc) + b_fc_in
    hidden = gelu_tanh(hidden_pre).astype(jnp.bfloat16)
    joined = jnp.concatenate([attn, hidden], axis=1)
    part = lax.dot_general(
        joined,
        gathered[:, n_in:],
        (((1,), (1,)), ((), ())),
        preferred_element_type=jnp.float32,
    )
    n_c = 2
    n_y = lax.axis_size("mlp") // n_c
    grid = part.reshape(tok, n_y, n_c, width_m)
    first = lax.axis_index("mlp") % n_c == 0
    keep = jnp.where(first, grid[:, :, 0, :], grid[:, :, 1, :])
    send = jnp.where(first, grid[:, :, 1, :], grid[:, :, 0, :])
    mates = [(i, i ^ 1) for i in range(n_y * n_c)]
    got = lax.ppermute(send, "mlp", mates)
    lanes = [[y * n_c + c for y in range(n_y)] for c in range(n_c)]
    shares = lax.psum_scatter(
        keep + got, "mlp", scatter_dimension=1, tiled=True, axis_index_groups=lanes
    )
    shares = shares.reshape(tok, width_m)
    result = (own_x.astype(jnp.float32) + shares + b_fc_out).astype(jnp.bfloat16)
    back_flat = result.reshape(pg_dev, page_len * width_m)
    leaving = jnp.dot(take.T, back_flat, preferred_element_type=jnp.float32).astype(jnp.bfloat16)
    leaving = leaving.reshape(groups, per_owner, page_len * width_m)
    returned = lax.all_to_all(leaving, "req", split_axis=0, concat_axis=0, tiled=True)
    pages_back = jnp.dot(
        place.T, returned.reshape(slots, page_len * width_m), preferred_element_type=jnp.float32
    )
    return pages_back.astype(jnp.bfloat16).reshape(pg_dev, page_len, width_m)


def solution(mesh):
    in_specs = (
        P("req", None, "mlp"),
        P("req"),
        P("req"),
        P("req"),
        P(),
        P(),
        P("req", "mlp"),
        P("req", "mlp"),
        P("req", "mlp"),
        P("mlp", "req"),
        P("mlp", None),
        P(None, "mlp"),
        P("mlp", None),
        P(None, "mlp"),
        P("req", "mlp"),
        P("mlp"),
        P("mlp", None),
        P(None, "mlp"),
        P("mlp", "req"),
        P("mlp"),
    )
    out_specs = P("req", None, "mlp")
    return jax.shard_map(
        on_device, mesh=mesh, in_specs=in_specs, out_specs=out_specs, check_vma=False
    )
```

```python
import jax
import jax.numpy as jnp
from jax import lax
from jax.experimental import pallas as pl
from jax.experimental.pallas import tpu as pltpu
from jax.sharding import PartitionSpec as P

HS = 256
ROT = 64
NAD = 64
R = 16


EPS = 1e-05


def gelu_tanh(v):
    return 0.5 * v * (1.0 + jnp.tanh(0.7978845608028654 * (v + 0.044715 * v * v * v)))


def rotate(block, pos):
    half = ROT // 2
    freq = jnp.power(10000.0, -jnp.arange(half).astype(jnp.float32) * 2.0 / ROT)
    angle = pos.astype(jnp.float32)[:, None, None] * freq[None, None, :]
    cosine = jnp.cos(angle)
    sine = jnp.sin(angle)
    even = block[:, :, 0:ROT:2]
    odd = block[:, :, 1:ROT:2]
    turned = jnp.stack([even * cosine - odd * sine, odd * cosine + even * sine], axis=-1)
    turned = turned.reshape(block.shape[0], block.shape[1], ROT)
    return jnp.concatenate([turned, block[:, :, ROT:]], axis=2)


def rotate_split(block, pos):
    half = ROT // 2
    freq = jnp.power(10000.0, -jnp.arange(half).astype(jnp.float32) * 2.0 / ROT)
    angle = pos.astype(jnp.float32)[:, None, None] * freq[None, None, :]
    cosine = jnp.cos(angle)
    sine = jnp.sin(angle)
    even = block[:, :, :half]
    odd = block[:, :, half:ROT]
    return jnp.concatenate(
        [even * cosine - odd * sine, odd * cosine + even * sine, block[:, :, ROT:]], axis=2
    )


def pack_kernel(wq_ref, wk_ref, wv_ref, wfi_ref, wao_ref, wfo_ref, out_ref):
    hw = wq_ref.shape[1]
    ff = wfi_ref.shape[1]
    rows = wq_ref.shape[0]
    src = lax.broadcasted_iota(jnp.int32, (hw, hw), 0)
    dst = lax.broadcasted_iota(jnp.int32, (hw, hw), 1)
    half = ROT // 2
    origin = jnp.where(
        dst < half, 2 * dst, jnp.where(dst < ROT, 2 * (dst - half) + 1, dst)
    )
    perm = (src == origin).astype(jnp.bfloat16)
    ident = (
        lax.broadcasted_iota(jnp.int32, (rows, rows), 0)
        == lax.broadcasted_iota(jnp.int32, (rows, rows), 1)
    ).astype(jnp.bfloat16)
    nt = (((1,), (1,)), ((), ()))
    out_ref[:, 0:hw] = jnp.dot(
        wq_ref[...], perm, preferred_element_type=jnp.float32
    ).astype(out_ref.dtype)
    out_ref[:, hw : 2 * hw] = jnp.dot(
        wk_ref[...], perm, preferred_element_type=jnp.float32
    ).astype(out_ref.dtype)
    out_ref[:, 2 * hw : 3 * hw] = wv_ref[...]
    out_ref[:, 3 * hw : 3 * hw + ff] = wfi_ref[...]
    base = 3 * hw + ff
    n_ao = wao_ref.shape[0]
    out_ref[:, base : base + n_ao] = lax.dot_general(
        ident, wao_ref[...], nt, preferred_element_type=jnp.float32
    ).astype(out_ref.dtype)
    n_fo = wfo_ref.shape[0]
    out_ref[:, base + n_ao : base + n_ao + n_fo] = lax.dot_general(
        ident, wfo_ref[...], nt, preferred_element_type=jnp.float32
    ).astype(out_ref.dtype)


def pack_weights(wq, wk, wv, wfi, wao, wfo):
    rows = wq.shape[0]
    cols = 3 * wq.shape[1] + wfi.shape[1] + wao.shape[0] + wfo.shape[0]
    vmem = pl.BlockSpec(memory_space=pltpu.VMEM)
    return pl.pallas_call(
        pack_kernel,
        out_shape=jax.ShapeDtypeStruct((rows, cols), wq.dtype),
        in_specs=[vmem] * 6,
        out_specs=vmem,
        cost_estimate=pl.CostEstimate(
            flops=2 * rows * (2 * wq.shape[1] ** 2 + rows * (wao.shape[0] + wfo.shape[0])),
            bytes_accessed=4 * rows * cols,
            transcendentals=0,
        ),
    )(wq, wk, wv, wfi, wao, wfo)


def on_device(
    x_pages,
    page_owner,
    request_id,
    adapter_table,
    ln_gain,
    ln_bias,
    w_query,
    w_key,
    w_value,
    w_attn_out,
    down_query,
    up_query,
    down_value,
    up_value,
    w_fc_in,
    b_fc_in,
    down_fc,
    up_fc,
    w_fc_out,
    b_fc_out,
):
    groups = lax.axis_size("req")
    pg_dev = x_pages.shape[0]
    page_len = x_pages.shape[1]
    width_m = x_pages.shape[2]
    tok = request_id.shape[0]
    per_owner = pg_dev // groups + 1
    slots = groups * per_owner
    page_iota = jnp.arange(pg_dev)
    earlier = (page_owner[None, :] == page_owner[:, None]) & (
        page_iota[None, :] < page_iota[:, None]
    )
    rank = jnp.sum(earlier.astype(jnp.int32), axis=1)
    slot = page_owner * per_owner + rank
    place = (slot[None, :] == jnp.arange(slots)[:, None]).astype(jnp.bfloat16)
    flat_pages = x_pages.reshape(pg_dev, page_len * width_m)
    outgoing = jnp.dot(place, flat_pages, preferred_element_type=jnp.float32).astype(jnp.bfloat16)
    outgoing = outgoing.reshape(groups, per_owner, page_len * width_m)
    filled = jnp.sum(place, axis=1).reshape(groups, per_owner)
    arrived, marks = (
        lax.all_to_all(outgoing, "req", split_axis=0, concat_axis=0, tiled=True),
        lax.all_to_all(filled, "req", split_axis=0, concat_axis=0, tiled=True),
    )
    valid = marks.reshape(slots).astype(jnp.float32)
    position = jnp.cumsum(valid) - 1.0
    take = (
        (position[None, :] == jnp.arange(pg_dev).astype(jnp.float32)[:, None])
        & (valid[None, :] > 0.5)
    ).astype(jnp.bfloat16)
    own_x = jnp.dot(
        take, arrived.reshape(slots, page_len * width_m), preferred_element_type=jnp.float32
    )
    own_x = own_x.astype(jnp.bfloat16).reshape(tok, width_m)
    column = lax.axis_index("mlp") * width_m
    n_mlp = lax.axis_size("mlp")
    copies = jnp.broadcast_to(own_x[None], (n_mlp, tok, width_m))
    spread_x = lax.all_to_all(copies, "mlp", split_axis=0, concat_axis=0, tiled=True)
    whole = jnp.transpose(spread_x, (1, 0, 2)).reshape(tok, n_mlp * width_m).astype(jnp.float32)
    mean = jnp.mean(whole, axis=1, keepdims=True)
    var = jnp.mean(jnp.square(whole - mean), axis=1, keepdims=True)
    full_ln = ((whole - mean) * lax.rsqrt(var + EPS) * ln_gain + ln_bias).astype(jnp.bfloat16)
    ln_m = lax.dynamic_slice_in_dim(full_ln, column, width_m, 1)
    local_req = request_id - lax.axis_index("req") * tok
    lookup = local_req[:, None] == jnp.arange(tok)[None, :]
    adapter = jnp.sum(jnp.where(lookup, adapter_table[None, :], 0), axis=1)
    onehot = (adapter[:, None] == jnp.arange(NAD)[None, :]).astype(jnp.float32)
    onehot_low = onehot.astype(jnp.bfloat16)

    def pick(down):
        spread = jnp.dot(ln_m, down, preferred_element_type=jnp.float32).reshape(tok, NAD, R)
        return jnp.sum(spread * onehot[:, :, None], axis=1)

    picked = lax.psum((pick(down_query), pick(down_value), pick(down_fc)), "mlp")

    def lift(chosen, up):
        expanded = (onehot_low[:, :, None] * chosen.astype(jnp.bfloat16)[:, None, :]).reshape(
            tok, NAD * R
        )
        return jnp.dot(expanded, up, preferred_element_type=jnp.float32)

    row_iota = jnp.arange(tok)
    start = jnp.sum((request_id[None, :] < request_id[:, None]).astype(jnp.int32), axis=1)
    pos = row_iota - start
    mask = (request_id[:, None] == request_id[None, :]) & (row_iota[None, :] <= row_iota[:, None])
    heads_w = w_query.shape[1]
    ff_w = w_fc_in.shape[1]
    def pair_major(w):
        rows = w.shape[0]
        lead = w[:, :ROT].reshape(rows, ROT // 2, 2).transpose(0, 2, 1).reshape(rows, ROT)
        return jnp.concatenate([lead, w[:, ROT:]], axis=1)

    packed = pack_weights(w_query, w_key, w_value, w_fc_in, w_attn_out, w_fc_out)
    gathered = lax.all_gather(packed, "req", axis=0, tiled=True)
    n_in = 3 * heads_w + ff_w
    base = jnp.dot(full_ln, gathered[:, :n_in], preferred_element_type=jnp.float32)
    base_q = base[:, :heads_w]
    base_k = base[:, heads_w : 2 * heads_w]
    base_v = base[:, 2 * heads_w : 3 * heads_w]
    query = rotate_split(
        (base_q + lift(picked[0], pair_major(up_query))).reshape(tok, heads_w // HS, HS), pos
    ).astype(jnp.bfloat16)
    keys = rotate_split(base_k.reshape(tok, heads_w // HS, HS), pos).astype(jnp.bfloat16)
    value = (
        (base_v + lift(picked[1], up_value)).astype(jnp.bfloat16).reshape(tok, heads_w // HS, HS)
    )
    scores = jnp.einsum("qhd,khd->hqk", query, keys, preferred_element_type=jnp.float32) * HS ** (
        -0.5
    )
    scores = jnp.where(mask[None, :, :], scores, -1e30)
    top = jnp.max(scores, axis=2, keepdims=True)
    weights = jnp.exp(scores - top)
    probs = (weights / jnp.sum(weights, axis=2, keepdims=True)).astype(jnp.bfloat16)
    mixed_heads = jnp.einsum("hqk,khd->qhd", probs, value, preferred_element_type=jnp.float32)
    attn = mixed_heads.astype(jnp.bfloat16).reshape(tok, heads_w)
    hidden_pre = base[:, 3 * heads_w :]
    hidden_pre = hidden_pre + lift(picked[2], up_fc) + b_fc_in
    hidden = gelu_tanh(hidden_pre).astype(jnp.bfloat16)
    joined = jnp.concatenate([attn, hidden], axis=1)
    n_c = 2
    n_y = lax.axis_size("mlp") // n_c
    w_out = gathered[:, n_in:].reshape(n_y, n_c, width_m, joined.shape[1])
    halves = [
        jnp.einsum("tk,yfk->tyf", joined, w_out[:, c], preferred_element_type=jnp.float32)
        for c in range(n_c)
    ]
    first = lax.axis_index("mlp") % n_c == 0
    keep = jnp.where(first, halves[0], halves[1])
    send = jnp.where(first, halves[1], halves[0])
    mates = [(i, i ^ 1) for i in range(n_y * n_c)]
    got = lax.ppermute(send, "mlp", mates)
    lanes = [[y * n_c + c for y in range(n_y)] for c in range(n_c)]
    shares = lax.psum_scatter(
        keep + got, "mlp", scatter_dimension=1, tiled=True, axis_index_groups=lanes
    )
    shares = shares.reshape(tok, width_m)
    result = (own_x.astype(jnp.float32) + shares + b_fc_out).astype(jnp.bfloat16)
    back_flat = result.reshape(pg_dev, page_len * width_m)
    leaving = jnp.dot(take.T, back_flat, preferred_element_type=jnp.float32).astype(jnp.bfloat16)
    leaving = leaving.reshape(groups, per_owner, page_len * width_m)
    returned = lax.all_to_all(leaving, "req", split_axis=0, concat_axis=0, tiled=True)
    pages_back = jnp.dot(
        place.T, returned.reshape(slots, page_len * width_m), preferred_element_type=jnp.float32
    )
    return pages_back.astype(jnp.bfloat16).reshape(pg_dev, page_len, width_m)


def solution(mesh):
    in_specs = (
        P("req", None, "mlp"),
        P("req"),
        P("req"),
        P("req"),
        P(),
        P(),
        P("req", "mlp"),
        P("req", "mlp"),
        P("req", "mlp"),
        P("mlp", "req"),
        P("mlp", None),
        P(None, "mlp"),
        P("mlp", None),
        P(None, "mlp"),
        P("req", "mlp"),
        P("mlp"),
        P("mlp", None),
        P(None, "mlp"),
        P("mlp", "req"),
        P("mlp"),
    )
    out_specs = P("req", None, "mlp")
    return jax.shard_map(
        on_device, mesh=mesh, in_specs=in_specs, out_specs=out_specs, check_vma=False
    )
```

```python
import jax
import jax.numpy as jnp
from jax import lax
from jax.experimental import pallas as pl
from jax.experimental.pallas import tpu as pltpu
from jax.sharding import PartitionSpec as P

HS = 256
ROT = 64
NAD = 64
R = 16


EPS = 1e-05


def gelu_tanh(v):
    return 0.5 * v * (1.0 + jnp.tanh(0.7978845608028654 * (v + 0.044715 * v * v * v)))


def rotate(block, pos):
    half = ROT // 2
    freq = jnp.power(10000.0, -jnp.arange(half).astype(jnp.float32) * 2.0 / ROT)
    angle = pos.astype(jnp.float32)[:, None, None] * freq[None, None, :]
    cosine = jnp.cos(angle)
    sine = jnp.sin(angle)
    even = block[:, :, 0:ROT:2]
    odd = block[:, :, 1:ROT:2]
    turned = jnp.stack([even * cosine - odd * sine, odd * cosine + even * sine], axis=-1)
    turned = turned.reshape(block.shape[0], block.shape[1], ROT)
    return jnp.concatenate([turned, block[:, :, ROT:]], axis=2)


def rotate_split(block, pos):
    half = ROT // 2
    freq = jnp.power(10000.0, -jnp.arange(half).astype(jnp.float32) * 2.0 / ROT)
    angle = pos.astype(jnp.float32)[:, None, None] * freq[None, None, :]
    cosine = jnp.cos(angle)
    sine = jnp.sin(angle)
    even = block[:, :, :half]
    odd = block[:, :, half:ROT]
    return jnp.concatenate(
        [even * cosine - odd * sine, odd * cosine + even * sine, block[:, :, ROT:]], axis=2
    )


def pack_kernel(wq_ref, wk_ref, wv_ref, wfi_ref, wao_ref, wfo_ref, out_ref):
    hw = wq_ref.shape[1]
    ff = wfi_ref.shape[1]
    rows = wq_ref.shape[0]
    src = lax.broadcasted_iota(jnp.int32, (hw, hw), 0)
    dst = lax.broadcasted_iota(jnp.int32, (hw, hw), 1)
    half = ROT // 2
    origin = jnp.where(
        dst < half, 2 * dst, jnp.where(dst < ROT, 2 * (dst - half) + 1, dst)
    )
    perm = (src == origin).astype(jnp.bfloat16)
    ident = (
        lax.broadcasted_iota(jnp.int32, (rows, rows), 0)
        == lax.broadcasted_iota(jnp.int32, (rows, rows), 1)
    ).astype(jnp.bfloat16)
    nt = (((1,), (1,)), ((), ()))
    out_ref[:, 0:hw] = jnp.dot(
        wq_ref[...], perm, preferred_element_type=jnp.float32
    ).astype(out_ref.dtype)
    out_ref[:, hw : 2 * hw] = jnp.dot(
        wk_ref[...], perm, preferred_element_type=jnp.float32
    ).astype(out_ref.dtype)
    out_ref[:, 2 * hw : 3 * hw] = wv_ref[...]
    out_ref[:, 3 * hw : 3 * hw + ff] = wfi_ref[...]
    base = 3 * hw + ff
    n_ao = wao_ref.shape[0]
    out_ref[:, base : base + n_ao] = lax.dot_general(
        ident, wao_ref[...], nt, preferred_element_type=jnp.float32
    ).astype(out_ref.dtype)
    n_fo = wfo_ref.shape[0]
    out_ref[:, base + n_ao : base + n_ao + n_fo] = lax.dot_general(
        ident, wfo_ref[...], nt, preferred_element_type=jnp.float32
    ).astype(out_ref.dtype)


def pack_weights(wq, wk, wv, wfi, wao, wfo):
    rows = wq.shape[0]
    cols = 3 * wq.shape[1] + wfi.shape[1] + wao.shape[0] + wfo.shape[0]
    vmem = pl.BlockSpec(memory_space=pltpu.VMEM)
    return pl.pallas_call(
        pack_kernel,
        out_shape=jax.ShapeDtypeStruct((rows, cols), wq.dtype),
        in_specs=[vmem] * 6,
        out_specs=vmem,
        cost_estimate=pl.CostEstimate(
            flops=2 * rows * (2 * wq.shape[1] ** 2 + rows * (wao.shape[0] + wfo.shape[0])),
            bytes_accessed=4 * rows * cols,
            transcendentals=0,
        ),
    )(wq, wk, wv, wfi, wao, wfo)


def project_kernel(a_ref, b_ref, o_ref):
    o_ref[...] = jnp.dot(a_ref[...], b_ref[...], preferred_element_type=jnp.float32)


def project(a, b, cols):
    rows, depth = a.shape
    tile = 256
    return pl.pallas_call(
        project_kernel,
        out_shape=jax.ShapeDtypeStruct((rows, cols), jnp.float32),
        grid=(cols // tile,),
        in_specs=[
            pl.BlockSpec((rows, depth), lambda j: (0, 0)),
            pl.BlockSpec((depth, tile), lambda j: (0, j)),
        ],
        out_specs=pl.BlockSpec((rows, tile), lambda j: (0, j)),
        cost_estimate=pl.CostEstimate(
            flops=2 * rows * depth * cols,
            bytes_accessed=2 * rows * depth + 2 * depth * cols + 4 * rows * cols,
            transcendentals=0,
        ),
    )(a, b)


def on_device(
    x_pages,
    page_owner,
    request_id,
    adapter_table,
    ln_gain,
    ln_bias,
    w_query,
    w_key,
    w_value,
    w_attn_out,
    down_query,
    up_query,
    down_value,
    up_value,
    w_fc_in,
    b_fc_in,
    down_fc,
    up_fc,
    w_fc_out,
    b_fc_out,
):
    groups = lax.axis_size("req")
    pg_dev = x_pages.shape[0]
    page_len = x_pages.shape[1]
    width_m = x_pages.shape[2]
    tok = request_id.shape[0]
    per_owner = pg_dev // groups + 1
    slots = groups * per_owner
    page_iota = jnp.arange(pg_dev)
    earlier = (page_owner[None, :] == page_owner[:, None]) & (
        page_iota[None, :] < page_iota[:, None]
    )
    rank = jnp.sum(earlier.astype(jnp.int32), axis=1)
    slot = page_owner * per_owner + rank
    place = (slot[None, :] == jnp.arange(slots)[:, None]).astype(jnp.bfloat16)
    flat_pages = x_pages.reshape(pg_dev, page_len * width_m)
    outgoing = jnp.dot(place, flat_pages, preferred_element_type=jnp.float32).astype(jnp.bfloat16)
    outgoing = outgoing.reshape(groups, per_owner, page_len * width_m)
    filled = jnp.sum(place, axis=1).reshape(groups, per_owner)
    arrived, marks = (
        lax.all_to_all(outgoing, "req", split_axis=0, concat_axis=0, tiled=True),
        lax.all_to_all(filled, "req", split_axis=0, concat_axis=0, tiled=True),
    )
    valid = marks.reshape(slots).astype(jnp.float32)
    position = jnp.cumsum(valid) - 1.0
    take = (
        (position[None, :] == jnp.arange(pg_dev).astype(jnp.float32)[:, None])
        & (valid[None, :] > 0.5)
    ).astype(jnp.bfloat16)
    own_x = jnp.dot(
        take, arrived.reshape(slots, page_len * width_m), preferred_element_type=jnp.float32
    )
    own_x = own_x.astype(jnp.bfloat16).reshape(tok, width_m)
    column = lax.axis_index("mlp") * width_m
    n_mlp = lax.axis_size("mlp")
    copies = jnp.broadcast_to(own_x[None], (n_mlp, tok, width_m))
    spread_x = lax.all_to_all(copies, "mlp", split_axis=0, concat_axis=0, tiled=True)
    whole = jnp.transpose(spread_x, (1, 0, 2)).reshape(tok, n_mlp * width_m).astype(jnp.float32)
    mean = jnp.mean(whole, axis=1, keepdims=True)
    var = jnp.mean(jnp.square(whole - mean), axis=1, keepdims=True)
    full_ln = ((whole - mean) * lax.rsqrt(var + EPS) * ln_gain + ln_bias).astype(jnp.bfloat16)
    ln_m = lax.dynamic_slice_in_dim(full_ln, column, width_m, 1)
    local_req = request_id - lax.axis_index("req") * tok
    lookup = local_req[:, None] == jnp.arange(tok)[None, :]
    adapter = jnp.sum(jnp.where(lookup, adapter_table[None, :], 0), axis=1)
    onehot = (adapter[:, None] == jnp.arange(NAD)[None, :]).astype(jnp.float32)
    onehot_low = onehot.astype(jnp.bfloat16)

    def pick(down):
        spread = jnp.dot(ln_m, down, preferred_element_type=jnp.float32).reshape(tok, NAD, R)
        return jnp.sum(spread * onehot[:, :, None], axis=1)

    picked = lax.psum((pick(down_query), pick(down_value), pick(down_fc)), "mlp")

    def lift(chosen, up):
        expanded = (onehot_low[:, :, None] * chosen.astype(jnp.bfloat16)[:, None, :]).reshape(
            tok, NAD * R
        )
        return jnp.dot(expanded, up, preferred_element_type=jnp.float32)

    row_iota = jnp.arange(tok)
    start = jnp.sum((request_id[None, :] < request_id[:, None]).astype(jnp.int32), axis=1)
    pos = row_iota - start
    mask = (request_id[:, None] == request_id[None, :]) & (row_iota[None, :] <= row_iota[:, None])
    heads_w = w_query.shape[1]
    ff_w = w_fc_in.shape[1]
    def pair_major(w):
        rows = w.shape[0]
        lead = w[:, :ROT].reshape(rows, ROT // 2, 2).transpose(0, 2, 1).reshape(rows, ROT)
        return jnp.concatenate([lead, w[:, ROT:]], axis=1)

    packed = pack_weights(w_query, w_key, w_value, w_fc_in, w_attn_out, w_fc_out)
    gathered = lax.all_gather(packed, "req", axis=0, tiled=True)
    n_in = 3 * heads_w + ff_w
    base = project(full_ln, gathered, n_in)
    base_q = base[:, :heads_w]
    base_k = base[:, heads_w : 2 * heads_w]
    base_v = base[:, 2 * heads_w : 3 * heads_w]
    query = rotate_split(
        (base_q + lift(picked[0], pair_major(up_query))).reshape(tok, heads_w // HS, HS), pos
    ).astype(jnp.bfloat16)
    keys = rotate_split(base_k.reshape(tok, heads_w // HS, HS), pos).astype(jnp.bfloat16)
    value = (
        (base_v + lift(picked[1], up_value)).astype(jnp.bfloat16).reshape(tok, heads_w // HS, HS)
    )
    scores = jnp.einsum("qhd,khd->hqk", query, keys, preferred_element_type=jnp.float32) * HS ** (
        -0.5
    )
    scores = jnp.where(mask[None, :, :], scores, -1e30)
    top = jnp.max(scores, axis=2, keepdims=True)
    weights = jnp.exp(scores - top)
    probs = (weights / jnp.sum(weights, axis=2, keepdims=True)).astype(jnp.bfloat16)
    mixed_heads = jnp.einsum("hqk,khd->qhd", probs, value, preferred_element_type=jnp.float32)
    attn = mixed_heads.astype(jnp.bfloat16).reshape(tok, heads_w)
    hidden_pre = base[:, 3 * heads_w :]
    hidden_pre = hidden_pre + lift(picked[2], up_fc) + b_fc_in
    hidden = gelu_tanh(hidden_pre).astype(jnp.bfloat16)
    joined = jnp.concatenate([attn, hidden], axis=1)
    part = lax.dot_general(
        joined,
        gathered[:, n_in:],
        (((1,), (1,)), ((), ())),
        preferred_element_type=jnp.float32,
    )
    shares = lax.psum_scatter(part, "mlp", scatter_dimension=1, tiled=True)
    result = (own_x.astype(jnp.float32) + shares + b_fc_out).astype(jnp.bfloat16)
    back_flat = result.reshape(pg_dev, page_len * width_m)
    leaving = jnp.dot(take.T, back_flat, preferred_element_type=jnp.float32).astype(jnp.bfloat16)
    leaving = leaving.reshape(groups, per_owner, page_len * width_m)
    returned = lax.all_to_all(leaving, "req", split_axis=0, concat_axis=0, tiled=True)
    pages_back = jnp.dot(
        place.T, returned.reshape(slots, page_len * width_m), preferred_element_type=jnp.float32
    )
    return pages_back.astype(jnp.bfloat16).reshape(pg_dev, page_len, width_m)


def solution(mesh):
    in_specs = (
        P("req", None, "mlp"),
        P("req"),
        P("req"),
        P("req"),
        P(),
        P(),
        P("req", "mlp"),
        P("req", "mlp"),
        P("req", "mlp"),
        P("mlp", "req"),
        P("mlp", None),
        P(None, "mlp"),
        P("mlp", None),
        P(None, "mlp"),
        P("req", "mlp"),
        P("mlp"),
        P("mlp", None),
        P(None, "mlp"),
        P("mlp", "req"),
        P("mlp"),
    )
    out_specs = P("req", None, "mlp")
    return jax.shard_map(
        on_device, mesh=mesh, in_specs=in_specs, out_specs=out_specs, check_vma=False
    )
```

```python
import jax
import jax.numpy as jnp
from jax import lax
from jax.experimental import pallas as pl
from jax.experimental.pallas import tpu as pltpu
from jax.sharding import PartitionSpec as P

HS = 256
ROT = 64
NAD = 64
R = 16


EPS = 1e-05


def gelu_tanh(v):
    return 0.5 * v * (1.0 + jnp.tanh(0.7978845608028654 * (v + 0.044715 * v * v * v)))


def rotate(block, pos):
    half = ROT // 2
    freq = jnp.power(10000.0, -jnp.arange(half).astype(jnp.float32) * 2.0 / ROT)
    angle = pos.astype(jnp.float32)[:, None, None] * freq[None, None, :]
    cosine = jnp.cos(angle)
    sine = jnp.sin(angle)
    even = block[:, :, 0:ROT:2]
    odd = block[:, :, 1:ROT:2]
    turned = jnp.stack([even * cosine - odd * sine, odd * cosine + even * sine], axis=-1)
    turned = turned.reshape(block.shape[0], block.shape[1], ROT)
    return jnp.concatenate([turned, block[:, :, ROT:]], axis=2)


def rotate_split(block, pos):
    half = ROT // 2
    freq = jnp.power(10000.0, -jnp.arange(half).astype(jnp.float32) * 2.0 / ROT)
    angle = pos.astype(jnp.float32)[:, None, None] * freq[None, None, :]
    cosine = jnp.cos(angle)
    sine = jnp.sin(angle)
    even = block[:, :, :half]
    odd = block[:, :, half:ROT]
    return jnp.concatenate(
        [even * cosine - odd * sine, odd * cosine + even * sine, block[:, :, ROT:]], axis=2
    )


def pack_kernel(wq_ref, wk_ref, wv_ref, wfi_ref, wao_ref, wfo_ref, out_ref):
    hw = wq_ref.shape[1]
    ff = wfi_ref.shape[1]
    rows = wq_ref.shape[0]
    src = lax.broadcasted_iota(jnp.int32, (hw, hw), 0)
    dst = lax.broadcasted_iota(jnp.int32, (hw, hw), 1)
    half = ROT // 2
    origin = jnp.where(
        dst < half, 2 * dst, jnp.where(dst < ROT, 2 * (dst - half) + 1, dst)
    )
    perm = (src == origin).astype(jnp.bfloat16)
    ident = (
        lax.broadcasted_iota(jnp.int32, (rows, rows), 0)
        == lax.broadcasted_iota(jnp.int32, (rows, rows), 1)
    ).astype(jnp.bfloat16)
    nt = (((1,), (1,)), ((), ()))
    out_ref[:, 0:hw] = jnp.dot(
        wq_ref[...], perm, preferred_element_type=jnp.float32
    ).astype(out_ref.dtype)
    out_ref[:, hw : 2 * hw] = jnp.dot(
        wk_ref[...], perm, preferred_element_type=jnp.float32
    ).astype(out_ref.dtype)
    out_ref[:, 2 * hw : 3 * hw] = wv_ref[...]
    out_ref[:, 3 * hw : 3 * hw + ff] = wfi_ref[...]
    base = 3 * hw + ff
    n_ao = wao_ref.shape[0]
    out_ref[:, base : base + n_ao] = lax.dot_general(
        ident, wao_ref[...], nt, preferred_element_type=jnp.float32
    ).astype(out_ref.dtype)
    n_fo = wfo_ref.shape[0]
    out_ref[:, base + n_ao : base + n_ao + n_fo] = lax.dot_general(
        ident, wfo_ref[...], nt, preferred_element_type=jnp.float32
    ).astype(out_ref.dtype)


def pack_weights(wq, wk, wv, wfi, wao, wfo):
    rows = wq.shape[0]
    cols = 3 * wq.shape[1] + wfi.shape[1] + wao.shape[0] + wfo.shape[0]
    vmem = pl.BlockSpec(memory_space=pltpu.VMEM)
    return pl.pallas_call(
        pack_kernel,
        out_shape=jax.ShapeDtypeStruct((rows, cols), wq.dtype),
        in_specs=[vmem] * 6,
        out_specs=vmem,
        cost_estimate=pl.CostEstimate(
            flops=2 * rows * (2 * wq.shape[1] ** 2 + rows * (wao.shape[0] + wfo.shape[0])),
            bytes_accessed=4 * rows * cols,
            transcendentals=0,
        ),
    )(wq, wk, wv, wfi, wao, wfo)


def on_device(
    x_pages,
    page_owner,
    request_id,
    adapter_table,
    ln_gain,
    ln_bias,
    w_query,
    w_key,
    w_value,
    w_attn_out,
    down_query,
    up_query,
    down_value,
    up_value,
    w_fc_in,
    b_fc_in,
    down_fc,
    up_fc,
    w_fc_out,
    b_fc_out,
):
    groups = lax.axis_size("req")
    pg_dev = x_pages.shape[0]
    page_len = x_pages.shape[1]
    width_m = x_pages.shape[2]
    tok = request_id.shape[0]
    per_owner = pg_dev // groups + 1
    slots = groups * per_owner
    page_iota = jnp.arange(pg_dev)
    earlier = (page_owner[None, :] == page_owner[:, None]) & (
        page_iota[None, :] < page_iota[:, None]
    )
    rank = jnp.sum(earlier.astype(jnp.int32), axis=1)
    slot = page_owner * per_owner + rank
    place = (slot[None, :] == jnp.arange(slots)[:, None]).astype(jnp.bfloat16)
    flat_pages = x_pages.reshape(pg_dev, page_len * width_m)
    outgoing = jnp.dot(place, flat_pages, preferred_element_type=jnp.float32).astype(jnp.bfloat16)
    outgoing = outgoing.reshape(groups, per_owner, page_len * width_m)
    filled = jnp.sum(place, axis=1).reshape(groups, per_owner)
    arrived, marks = (
        lax.all_to_all(outgoing, "req", split_axis=0, concat_axis=0, tiled=True),
        lax.all_to_all(filled, "req", split_axis=0, concat_axis=0, tiled=True),
    )
    valid = marks.reshape(slots).astype(jnp.float32)
    position = jnp.cumsum(valid) - 1.0
    take = (
        (position[None, :] == jnp.arange(pg_dev).astype(jnp.float32)[:, None])
        & (valid[None, :] > 0.5)
    ).astype(jnp.bfloat16)
    own_x = jnp.dot(
        take, arrived.reshape(slots, page_len * width_m), preferred_element_type=jnp.float32
    )
    own_x = own_x.astype(jnp.bfloat16).reshape(tok, width_m)
    column = lax.axis_index("mlp") * width_m
    n_mlp = lax.axis_size("mlp")
    copies = jnp.broadcast_to(own_x[None], (n_mlp, tok, width_m))
    spread_x = lax.all_to_all(copies, "mlp", split_axis=0, concat_axis=0, tiled=True)
    whole = jnp.transpose(spread_x, (1, 0, 2)).reshape(tok, n_mlp * width_m).astype(jnp.float32)
    mean = jnp.mean(whole, axis=1, keepdims=True)
    var = jnp.mean(jnp.square(whole - mean), axis=1, keepdims=True)
    full_ln = ((whole - mean) * lax.rsqrt(var + EPS) * ln_gain + ln_bias).astype(jnp.bfloat16)
    ln_m = lax.dynamic_slice_in_dim(full_ln, column, width_m, 1)
    local_req = request_id - lax.axis_index("req") * tok
    lookup = local_req[:, None] == jnp.arange(tok)[None, :]
    adapter = jnp.sum(jnp.where(lookup, adapter_table[None, :], 0), axis=1)
    onehot = (adapter[:, None] == jnp.arange(NAD)[None, :]).astype(jnp.float32)
    onehot_low = onehot.astype(jnp.bfloat16)

    def pick(down):
        spread = jnp.dot(ln_m, down, preferred_element_type=jnp.float32).reshape(tok, NAD, R)
        return jnp.sum(spread * onehot[:, :, None], axis=1)

    picked = lax.psum((pick(down_query), pick(down_value), pick(down_fc)), "mlp")

    def lift(chosen, up):
        expanded = (onehot_low[:, :, None] * chosen.astype(jnp.bfloat16)[:, None, :]).reshape(
            tok, NAD * R
        )
        return jnp.dot(expanded, up, preferred_element_type=jnp.float32)

    row_iota = jnp.arange(tok)
    start = jnp.sum((request_id[None, :] < request_id[:, None]).astype(jnp.int32), axis=1)
    pos = row_iota - start
    mask = (request_id[:, None] == request_id[None, :]) & (row_iota[None, :] <= row_iota[:, None])
    heads_w = w_query.shape[1]
    ff_w = w_fc_in.shape[1]
    def pair_major(w):
        rows = w.shape[0]
        lead = w[:, :ROT].reshape(rows, ROT // 2, 2).transpose(0, 2, 1).reshape(rows, ROT)
        return jnp.concatenate([lead, w[:, ROT:]], axis=1)

    packed = pack_weights(w_query, w_key, w_value, w_fc_in, w_attn_out, w_fc_out)
    gathered = lax.all_gather(packed, "req", axis=0, tiled=True)
    n_in = 3 * heads_w + ff_w
    base = jnp.dot(full_ln, gathered[:, :n_in], preferred_element_type=jnp.float32)
    base_q = base[:, :heads_w]
    base_k = base[:, heads_w : 2 * heads_w]
    base_v = base[:, 2 * heads_w : 3 * heads_w]
    query = rotate_split(
        (base_q + lift(picked[0], pair_major(up_query))).reshape(tok, heads_w // HS, HS), pos
    ).astype(jnp.bfloat16)
    keys = rotate_split(base_k.reshape(tok, heads_w // HS, HS), pos).astype(jnp.bfloat16)
    value = (
        (base_v + lift(picked[1], up_value)).astype(jnp.bfloat16).reshape(tok, heads_w // HS, HS)
    )
    scores = jnp.einsum("qhd,khd->hqk", query, keys, preferred_element_type=jnp.float32) * HS ** (
        -0.5
    )
    scores = jnp.where(mask[None, :, :], scores, -1e30)
    top = jnp.max(scores, axis=2, keepdims=True)
    weights = jnp.exp(scores - top)
    probs = (weights / jnp.sum(weights, axis=2, keepdims=True)).astype(jnp.bfloat16)
    mixed_heads = jnp.einsum("hqk,khd->qhd", probs, value, preferred_element_type=jnp.float32)
    attn = mixed_heads.astype(jnp.bfloat16).reshape(tok, heads_w)
    hidden_pre = base[:, 3 * heads_w :]
    hidden_pre = hidden_pre + lift(picked[2], up_fc) + b_fc_in
    hidden = gelu_tanh(hidden_pre).astype(jnp.bfloat16)
    joined = jnp.concatenate([attn, hidden], axis=1)
    part = lax.dot_general(
        joined,
        gathered[:, n_in:],
        (((1,), (1,)), ((), ())),
        preferred_element_type=jnp.float32,
    )
    shares = lax.psum_scatter(part, "mlp", scatter_dimension=1, tiled=True)
    result = (own_x.astype(jnp.float32) + shares + b_fc_out).astype(jnp.bfloat16)
    back_flat = result.reshape(pg_dev, page_len * width_m)
    leaving = jnp.dot(take.T, back_flat, preferred_element_type=jnp.float32).astype(jnp.bfloat16)
    leaving = leaving.reshape(groups, per_owner, page_len * width_m)
    returned = lax.all_to_all(leaving, "req", split_axis=0, concat_axis=0, tiled=True)
    pages_back = jnp.einsum(
        "pab,abk->pk",
        place.T.reshape(pg_dev, groups, per_owner),
        returned,
        preferred_element_type=jnp.float32,
    )
    return pages_back.astype(jnp.bfloat16).reshape(pg_dev, page_len, width_m)


def solution(mesh):
    in_specs = (
        P("req", None, "mlp"),
        P("req"),
        P("req"),
        P("req"),
        P(),
        P(),
        P("req", "mlp"),
        P("req", "mlp"),
        P("req", "mlp"),
        P("mlp", "req"),
        P("mlp", None),
        P(None, "mlp"),
        P("mlp", None),
        P(None, "mlp"),
        P("req", "mlp"),
        P("mlp"),
        P("mlp", None),
        P(None, "mlp"),
        P("mlp", "req"),
        P("mlp"),
    )
    out_specs = P("req", None, "mlp")
    return jax.shard_map(
        on_device, mesh=mesh, in_specs=in_specs, out_specs=out_specs, check_vma=False
    )
```

```python
import jax
import jax.numpy as jnp
from jax import lax
from jax.experimental import pallas as pl
from jax.experimental.pallas import tpu as pltpu
from jax.sharding import PartitionSpec as P

HS = 256
ROT = 64
NAD = 64
R = 16


EPS = 1e-05


def gelu_tanh(v):
    return 0.5 * v * (1.0 + jnp.tanh(0.7978845608028654 * (v + 0.044715 * v * v * v)))


def rotate(block, pos):
    half = ROT // 2
    freq = jnp.power(10000.0, -jnp.arange(half).astype(jnp.float32) * 2.0 / ROT)
    angle = pos.astype(jnp.float32)[:, None, None] * freq[None, None, :]
    cosine = jnp.cos(angle)
    sine = jnp.sin(angle)
    even = block[:, :, 0:ROT:2]
    odd = block[:, :, 1:ROT:2]
    turned = jnp.stack([even * cosine - odd * sine, odd * cosine + even * sine], axis=-1)
    turned = turned.reshape(block.shape[0], block.shape[1], ROT)
    return jnp.concatenate([turned, block[:, :, ROT:]], axis=2)


def rotate_split(block, pos):
    half = ROT // 2
    freq = jnp.power(10000.0, -jnp.arange(half).astype(jnp.float32) * 2.0 / ROT)
    angle = pos.astype(jnp.float32)[:, None, None] * freq[None, None, :]
    cosine = jnp.cos(angle)
    sine = jnp.sin(angle)
    even = block[:, :, :half]
    odd = block[:, :, half:ROT]
    return jnp.concatenate(
        [even * cosine - odd * sine, odd * cosine + even * sine, block[:, :, ROT:]], axis=2
    )


def pack_kernel(wq_ref, wk_ref, wv_ref, wfi_ref, wao_ref, wfo_ref, out_ref):
    hw = wq_ref.shape[1]
    ff = wfi_ref.shape[1]
    rows = wq_ref.shape[0]
    src = lax.broadcasted_iota(jnp.int32, (hw, hw), 0)
    dst = lax.broadcasted_iota(jnp.int32, (hw, hw), 1)
    half = ROT // 2
    origin = jnp.where(
        dst < half, 2 * dst, jnp.where(dst < ROT, 2 * (dst - half) + 1, dst)
    )
    perm = (src == origin).astype(jnp.bfloat16)
    ident = (
        lax.broadcasted_iota(jnp.int32, (rows, rows), 0)
        == lax.broadcasted_iota(jnp.int32, (rows, rows), 1)
    ).astype(jnp.bfloat16)
    nt = (((1,), (1,)), ((), ()))
    out_ref[:, 0:hw] = jnp.dot(
        wq_ref[...], perm, preferred_element_type=jnp.float32
    ).astype(out_ref.dtype)
    out_ref[:, hw : 2 * hw] = jnp.dot(
        wk_ref[...], perm, preferred_element_type=jnp.float32
    ).astype(out_ref.dtype)
    out_ref[:, 2 * hw : 3 * hw] = wv_ref[...]
    out_ref[:, 3 * hw : 3 * hw + ff] = wfi_ref[...]
    base = 3 * hw + ff
    n_ao = wao_ref.shape[0]
    out_ref[:, base : base + n_ao] = wao_ref[...].T
    n_fo = wfo_ref.shape[0]
    out_ref[:, base + n_ao : base + n_ao + n_fo] = wfo_ref[...].T


def pack_weights(wq, wk, wv, wfi, wao, wfo):
    rows = wq.shape[0]
    cols = 3 * wq.shape[1] + wfi.shape[1] + wao.shape[0] + wfo.shape[0]
    vmem = pl.BlockSpec(memory_space=pltpu.VMEM)
    return pl.pallas_call(
        pack_kernel,
        out_shape=jax.ShapeDtypeStruct((rows, cols), wq.dtype),
        in_specs=[vmem] * 6,
        out_specs=vmem,
        cost_estimate=pl.CostEstimate(
            flops=2 * rows * (2 * wq.shape[1] ** 2 + rows * (wao.shape[0] + wfo.shape[0])),
            bytes_accessed=4 * rows * cols,
            transcendentals=0,
        ),
    )(wq, wk, wv, wfi, wao, wfo)


def on_device(
    x_pages,
    page_owner,
    request_id,
    adapter_table,
    ln_gain,
    ln_bias,
    w_query,
    w_key,
    w_value,
    w_attn_out,
    down_query,
    up_query,
    down_value,
    up_value,
    w_fc_in,
    b_fc_in,
    down_fc,
    up_fc,
    w_fc_out,
    b_fc_out,
):
    groups = lax.axis_size("req")
    pg_dev = x_pages.shape[0]
    page_len = x_pages.shape[1]
    width_m = x_pages.shape[2]
    tok = request_id.shape[0]
    per_owner = pg_dev // groups + 1
    slots = groups * per_owner
    page_iota = jnp.arange(pg_dev)
    earlier = (page_owner[None, :] == page_owner[:, None]) & (
        page_iota[None, :] < page_iota[:, None]
    )
    rank = jnp.sum(earlier.astype(jnp.int32), axis=1)
    slot = page_owner * per_owner + rank
    place = (slot[None, :] == jnp.arange(slots)[:, None]).astype(jnp.bfloat16)
    flat_pages = x_pages.reshape(pg_dev, page_len * width_m)
    outgoing = jnp.dot(place, flat_pages, preferred_element_type=jnp.float32).astype(jnp.bfloat16)
    outgoing = outgoing.reshape(groups, per_owner, page_len * width_m)
    filled = jnp.sum(place, axis=1).reshape(groups, per_owner)
    arrived, marks = (
        lax.all_to_all(outgoing, "req", split_axis=0, concat_axis=0, tiled=True),
        lax.all_to_all(filled, "req", split_axis=0, concat_axis=0, tiled=True),
    )
    valid = marks.reshape(slots).astype(jnp.float32)
    position = jnp.cumsum(valid) - 1.0
    take = (
        (position[None, :] == jnp.arange(pg_dev).astype(jnp.float32)[:, None])
        & (valid[None, :] > 0.5)
    ).astype(jnp.bfloat16)
    own_x = jnp.dot(
        take, arrived.reshape(slots, page_len * width_m), preferred_element_type=jnp.float32
    )
    own_x = own_x.astype(jnp.bfloat16).reshape(tok, width_m)
    column = lax.axis_index("mlp") * width_m
    n_mlp = lax.axis_size("mlp")
    copies = jnp.broadcast_to(own_x[None], (n_mlp, tok, width_m))
    spread_x = lax.all_to_all(copies, "mlp", split_axis=0, concat_axis=0, tiled=True)
    whole = jnp.transpose(spread_x, (1, 0, 2)).reshape(tok, n_mlp * width_m).astype(jnp.float32)
    mean = jnp.mean(whole, axis=1, keepdims=True)
    var = jnp.mean(jnp.square(whole - mean), axis=1, keepdims=True)
    full_ln = ((whole - mean) * lax.rsqrt(var + EPS) * ln_gain + ln_bias).astype(jnp.bfloat16)
    ln_m = lax.dynamic_slice_in_dim(full_ln, column, width_m, 1)
    local_req = request_id - lax.axis_index("req") * tok
    lookup = local_req[:, None] == jnp.arange(tok)[None, :]
    adapter = jnp.sum(jnp.where(lookup, adapter_table[None, :], 0), axis=1)
    onehot = (adapter[:, None] == jnp.arange(NAD)[None, :]).astype(jnp.float32)
    onehot_low = onehot.astype(jnp.bfloat16)

    def pick(down):
        spread = jnp.dot(ln_m, down, preferred_element_type=jnp.float32).reshape(tok, NAD, R)
        return jnp.sum(spread * onehot[:, :, None], axis=1)

    picked = lax.psum((pick(down_query), pick(down_value), pick(down_fc)), "mlp")

    def lift(chosen, up):
        expanded = (onehot_low[:, :, None] * chosen.astype(jnp.bfloat16)[:, None, :]).reshape(
            tok, NAD * R
        )
        return jnp.dot(expanded, up, preferred_element_type=jnp.float32)

    row_iota = jnp.arange(tok)
    start = jnp.sum((request_id[None, :] < request_id[:, None]).astype(jnp.int32), axis=1)
    pos = row_iota - start
    mask = (request_id[:, None] == request_id[None, :]) & (row_iota[None, :] <= row_iota[:, None])
    heads_w = w_query.shape[1]
    ff_w = w_fc_in.shape[1]
    def pair_major(w):
        rows = w.shape[0]
        lead = w[:, :ROT].reshape(rows, ROT // 2, 2).transpose(0, 2, 1).reshape(rows, ROT)
        return jnp.concatenate([lead, w[:, ROT:]], axis=1)

    packed = pack_weights(w_query, w_key, w_value, w_fc_in, w_attn_out, w_fc_out)
    gathered = lax.all_gather(packed, "req", axis=0, tiled=True)
    n_in = 3 * heads_w + ff_w
    base = jnp.dot(full_ln, gathered[:, :n_in], preferred_element_type=jnp.float32)
    base_q = base[:, :heads_w]
    base_k = base[:, heads_w : 2 * heads_w]
    base_v = base[:, 2 * heads_w : 3 * heads_w]
    query = rotate_split(
        (base_q + lift(picked[0], pair_major(up_query))).reshape(tok, heads_w // HS, HS), pos
    ).astype(jnp.bfloat16)
    keys = rotate_split(base_k.reshape(tok, heads_w // HS, HS), pos).astype(jnp.bfloat16)
    value = (
        (base_v + lift(picked[1], up_value)).astype(jnp.bfloat16).reshape(tok, heads_w // HS, HS)
    )
    scores = jnp.einsum("qhd,khd->hqk", query, keys, preferred_element_type=jnp.float32) * HS ** (
        -0.5
    )
    scores = jnp.where(mask[None, :, :], scores, -1e30)
    top = jnp.max(scores, axis=2, keepdims=True)
    weights = jnp.exp(scores - top)
    probs = (weights / jnp.sum(weights, axis=2, keepdims=True)).astype(jnp.bfloat16)
    mixed_heads = jnp.einsum("hqk,khd->qhd", probs, value, preferred_element_type=jnp.float32)
    attn = mixed_heads.astype(jnp.bfloat16).reshape(tok, heads_w)
    hidden_pre = base[:, 3 * heads_w :]
    hidden_pre = hidden_pre + lift(picked[2], up_fc) + b_fc_in
    hidden = gelu_tanh(hidden_pre).astype(jnp.bfloat16)
    joined = jnp.concatenate([attn, hidden], axis=1)
    part = lax.dot_general(
        joined,
        gathered[:, n_in:],
        (((1,), (1,)), ((), ())),
        preferred_element_type=jnp.float32,
    )
    shares = lax.psum_scatter(part, "mlp", scatter_dimension=1, tiled=True)
    result = (own_x.astype(jnp.float32) + shares + b_fc_out).astype(jnp.bfloat16)
    back_flat = result.reshape(pg_dev, page_len * width_m)
    leaving = jnp.dot(take.T, back_flat, preferred_element_type=jnp.float32).astype(jnp.bfloat16)
    leaving = leaving.reshape(groups, per_owner, page_len * width_m)
    returned = lax.all_to_all(leaving, "req", split_axis=0, concat_axis=0, tiled=True)
    pages_back = jnp.dot(
        place.T, returned.reshape(slots, page_len * width_m), preferred_element_type=jnp.float32
    )
    return pages_back.astype(jnp.bfloat16).reshape(pg_dev, page_len, width_m)


def solution(mesh):
    in_specs = (
        P("req", None, "mlp"),
        P("req"),
        P("req"),
        P("req"),
        P(),
        P(),
        P("req", "mlp"),
        P("req", "mlp"),
        P("req", "mlp"),
        P("mlp", "req"),
        P("mlp", None),
        P(None, "mlp"),
        P("mlp", None),
        P(None, "mlp"),
        P("req", "mlp"),
        P("mlp"),
        P("mlp", None),
        P(None, "mlp"),
        P("mlp", "req"),
        P("mlp"),
    )
    out_specs = P("req", None, "mlp")
    return jax.shard_map(
        on_device, mesh=mesh, in_specs=in_specs, out_specs=out_specs, check_vma=False
    )
```

```python
import jax
import jax.numpy as jnp
from jax import lax
from jax.experimental import pallas as pl
from jax.experimental.pallas import tpu as pltpu
from jax.sharding import PartitionSpec as P

HS = 256
ROT = 64
NAD = 64
R = 16


EPS = 1e-05


def gelu_tanh(v):
    return 0.5 * v * (1.0 + jnp.tanh(0.7978845608028654 * (v + 0.044715 * v * v * v)))


def rotate(block, pos):
    half = ROT // 2
    freq = jnp.power(10000.0, -jnp.arange(half).astype(jnp.float32) * 2.0 / ROT)
    angle = pos.astype(jnp.float32)[:, None, None] * freq[None, None, :]
    cosine = jnp.cos(angle)
    sine = jnp.sin(angle)
    even = block[:, :, 0:ROT:2]
    odd = block[:, :, 1:ROT:2]
    turned = jnp.stack([even * cosine - odd * sine, odd * cosine + even * sine], axis=-1)
    turned = turned.reshape(block.shape[0], block.shape[1], ROT)
    return jnp.concatenate([turned, block[:, :, ROT:]], axis=2)


def rotate_split(block, pos):
    half = ROT // 2
    freq = jnp.power(10000.0, -jnp.arange(half).astype(jnp.float32) * 2.0 / ROT)
    angle = pos.astype(jnp.float32)[:, None, None] * freq[None, None, :]
    cosine = jnp.cos(angle)
    sine = jnp.sin(angle)
    even = block[:, :, :half]
    odd = block[:, :, half:ROT]
    return jnp.concatenate(
        [even * cosine - odd * sine, odd * cosine + even * sine, block[:, :, ROT:]], axis=2
    )


def pack_kernel(wq_ref, wk_ref, wv_ref, wfi_ref, wao_ref, wfo_ref, out_ref):
    hw = wq_ref.shape[1]
    ff = wfi_ref.shape[1]
    rows = wq_ref.shape[0]
    src = lax.broadcasted_iota(jnp.int32, (hw, hw), 0)
    dst = lax.broadcasted_iota(jnp.int32, (hw, hw), 1)
    half = ROT // 2
    origin = jnp.where(
        dst < half, 2 * dst, jnp.where(dst < ROT, 2 * (dst - half) + 1, dst)
    )
    perm = (src == origin).astype(jnp.bfloat16)
    ident = (
        lax.broadcasted_iota(jnp.int32, (rows, rows), 0)
        == lax.broadcasted_iota(jnp.int32, (rows, rows), 1)
    ).astype(jnp.bfloat16)
    nt = (((1,), (1,)), ((), ()))
    out_ref[:, 0:hw] = jnp.dot(
        wq_ref[...], perm, preferred_element_type=jnp.float32
    ).astype(out_ref.dtype)
    out_ref[:, hw : 2 * hw] = jnp.dot(
        wk_ref[...], perm, preferred_element_type=jnp.float32
    ).astype(out_ref.dtype)
    out_ref[:, 2 * hw : 3 * hw] = wv_ref[...]
    out_ref[:, 3 * hw : 3 * hw + ff] = wfi_ref[...]
    base = 3 * hw + ff
    n_ao = wao_ref.shape[0]
    out_ref[:, base : base + n_ao] = lax.dot_general(
        ident, wao_ref[...], nt, preferred_element_type=jnp.float32
    ).astype(out_ref.dtype)
    n_fo = wfo_ref.shape[0]
    out_ref[:, base + n_ao : base + n_ao + n_fo] = lax.dot_general(
        ident, wfo_ref[...], nt, preferred_element_type=jnp.float32
    ).astype(out_ref.dtype)


def pack_weights(wq, wk, wv, wfi, wao, wfo):
    rows = wq.shape[0]
    cols = 3 * wq.shape[1] + wfi.shape[1] + wao.shape[0] + wfo.shape[0]
    vmem = pl.BlockSpec(memory_space=pltpu.VMEM)
    return pl.pallas_call(
        pack_kernel,
        out_shape=jax.ShapeDtypeStruct((rows, cols), wq.dtype),
        in_specs=[vmem] * 6,
        out_specs=vmem,
        cost_estimate=pl.CostEstimate(
            flops=2 * rows * (2 * wq.shape[1] ** 2 + rows * (wao.shape[0] + wfo.shape[0])),
            bytes_accessed=4 * rows * cols,
            transcendentals=0,
        ),
    )(wq, wk, wv, wfi, wao, wfo)


def on_device(
    x_pages,
    page_owner,
    request_id,
    adapter_table,
    ln_gain,
    ln_bias,
    w_query,
    w_key,
    w_value,
    w_attn_out,
    down_query,
    up_query,
    down_value,
    up_value,
    w_fc_in,
    b_fc_in,
    down_fc,
    up_fc,
    w_fc_out,
    b_fc_out,
):
    groups = lax.axis_size("req")
    pg_dev = x_pages.shape[0]
    page_len = x_pages.shape[1]
    width_m = x_pages.shape[2]
    tok = request_id.shape[0]
    per_owner = pg_dev // groups + 1
    slots = groups * per_owner
    page_iota = jnp.arange(pg_dev)
    earlier = (page_owner[None, :] == page_owner[:, None]) & (
        page_iota[None, :] < page_iota[:, None]
    )
    rank = jnp.sum(earlier.astype(jnp.int32), axis=1)
    slot = page_owner * per_owner + rank
    place = (slot[None, :] == jnp.arange(slots)[:, None]).astype(jnp.bfloat16)
    flat_pages = x_pages.reshape(pg_dev, page_len * width_m)
    outgoing = jnp.dot(place, flat_pages, preferred_element_type=jnp.float32).astype(jnp.bfloat16)
    outgoing = outgoing.reshape(groups, per_owner, page_len * width_m)
    filled = jnp.sum(place, axis=1).reshape(groups, per_owner)
    arrived, marks = (
        lax.all_to_all(outgoing, "req", split_axis=0, concat_axis=0, tiled=True),
        lax.all_to_all(filled, "req", split_axis=0, concat_axis=0, tiled=True),
    )
    valid = marks.reshape(slots).astype(jnp.float32)
    position = jnp.cumsum(valid) - 1.0
    take = (
        (position[None, :] == jnp.arange(pg_dev).astype(jnp.float32)[:, None])
        & (valid[None, :] > 0.5)
    ).astype(jnp.bfloat16)
    own_x = jnp.dot(
        take, arrived.reshape(slots, page_len * width_m), preferred_element_type=jnp.float32
    )
    own_x = own_x.astype(jnp.bfloat16).reshape(tok, width_m)
    column = lax.axis_index("mlp") * width_m
    n_mlp = lax.axis_size("mlp")
    copies = jnp.broadcast_to(own_x[None], (n_mlp, tok, width_m))
    spread_x = lax.all_to_all(copies, "mlp", split_axis=0, concat_axis=0, tiled=True)
    whole = jnp.transpose(spread_x, (1, 0, 2)).reshape(tok, n_mlp * width_m).astype(jnp.float32)
    mean = jnp.mean(whole, axis=1, keepdims=True)
    var = jnp.mean(jnp.square(whole - mean), axis=1, keepdims=True)
    full_ln = ((whole - mean) * lax.rsqrt(var + EPS) * ln_gain + ln_bias).astype(jnp.bfloat16)
    ln_m = lax.dynamic_slice_in_dim(full_ln, column, width_m, 1)
    local_req = request_id - lax.axis_index("req") * tok
    lookup = local_req[:, None] == jnp.arange(tok)[None, :]
    adapter = jnp.sum(jnp.where(lookup, adapter_table[None, :], 0), axis=1)
    onehot = (adapter[:, None] == jnp.arange(NAD)[None, :]).astype(jnp.float32)
    onehot_low = onehot.astype(jnp.bfloat16)

    def pick(down):
        spread = jnp.dot(ln_m, down, preferred_element_type=jnp.float32).reshape(tok, NAD, R)
        return jnp.sum(spread * onehot[:, :, None], axis=1)

    picked = lax.psum((pick(down_query), pick(down_value), pick(down_fc)), "mlp")

    def lift(chosen, up):
        expanded = (onehot_low[:, :, None] * chosen.astype(jnp.bfloat16)[:, None, :]).reshape(
            tok, NAD * R
        )
        return jnp.dot(expanded, up, preferred_element_type=jnp.float32)

    row_iota = jnp.arange(tok)
    start = jnp.sum((request_id[None, :] < request_id[:, None]).astype(jnp.int32), axis=1)
    pos = row_iota - start
    mask = (request_id[:, None] == request_id[None, :]) & (row_iota[None, :] <= row_iota[:, None])
    heads_w = w_query.shape[1]
    ff_w = w_fc_in.shape[1]
    def pair_major(w):
        rows = w.shape[0]
        lead = w[:, :ROT].reshape(rows, ROT // 2, 2).transpose(0, 2, 1).reshape(rows, ROT)
        return jnp.concatenate([lead, w[:, ROT:]], axis=1)

    packed = pack_weights(w_query, w_key, w_value, w_fc_in, w_attn_out, w_fc_out)
    gathered = lax.all_gather(packed, "req", axis=0, tiled=True)
    n_in = 3 * heads_w + ff_w
    base = jnp.dot(full_ln, gathered[:, :n_in], preferred_element_type=jnp.float32)
    base_q = base[:, :heads_w]
    base_k = base[:, heads_w : 2 * heads_w]
    base_v = base[:, 2 * heads_w : 3 * heads_w]
    query = rotate_split(
        (base_q + lift(picked[0], pair_major(up_query))).reshape(tok, heads_w // HS, HS), pos
    ).astype(jnp.bfloat16)
    keys = rotate_split(base_k.reshape(tok, heads_w // HS, HS), pos).astype(jnp.bfloat16)
    value = (
        (base_v + lift(picked[1], up_value)).astype(jnp.bfloat16).reshape(tok, heads_w // HS, HS)
    )
    scores = jnp.einsum("qhd,khd->hqk", query, keys, preferred_element_type=jnp.float32) * HS ** (
        -0.5
    )
    scores = jnp.where(mask[None, :, :], scores, -1e30)
    top = jnp.max(scores, axis=2, keepdims=True)
    weights = jnp.exp(scores - top)
    probs = (weights / jnp.sum(weights, axis=2, keepdims=True)).astype(jnp.bfloat16)
    mixed_heads = jnp.einsum("hqk,khd->qhd", probs, value, preferred_element_type=jnp.float32)
    attn = mixed_heads.astype(jnp.bfloat16).reshape(tok, heads_w)
    hidden_pre = base[:, 3 * heads_w :]
    hidden_pre = hidden_pre + lift(picked[2], up_fc) + b_fc_in
    hidden = gelu_tanh(hidden_pre).astype(jnp.bfloat16)
    joined = jnp.concatenate([attn, hidden], axis=1)
    part = lax.dot_general(
        joined,
        gathered[:, n_in:],
        (((1,), (1,)), ((), ())),
        preferred_element_type=jnp.float32,
    )
    n_out = lax.axis_size("mlp")
    mine = own_x.astype(jnp.float32) + b_fc_out
    owned = (jnp.arange(n_out * width_m) // width_m) == lax.axis_index("mlp")
    part = part + jnp.where(owned[None, :], jnp.tile(mine, (1, n_out)), 0.0)
    shares = lax.psum_scatter(part, "mlp", scatter_dimension=1, tiled=True)
    result = shares.astype(jnp.bfloat16)
    back_flat = result.reshape(pg_dev, page_len * width_m)
    leaving = jnp.dot(take.T, back_flat, preferred_element_type=jnp.float32).astype(jnp.bfloat16)
    leaving = leaving.reshape(groups, per_owner, page_len * width_m)
    returned = lax.all_to_all(leaving, "req", split_axis=0, concat_axis=0, tiled=True)
    pages_back = jnp.dot(
        place.T, returned.reshape(slots, page_len * width_m), preferred_element_type=jnp.float32
    )
    return pages_back.astype(jnp.bfloat16).reshape(pg_dev, page_len, width_m)


def solution(mesh):
    in_specs = (
        P("req", None, "mlp"),
        P("req"),
        P("req"),
        P("req"),
        P(),
        P(),
        P("req", "mlp"),
        P("req", "mlp"),
        P("req", "mlp"),
        P("mlp", "req"),
        P("mlp", None),
        P(None, "mlp"),
        P("mlp", None),
        P(None, "mlp"),
        P("req", "mlp"),
        P("mlp"),
        P("mlp", None),
        P(None, "mlp"),
        P("mlp", "req"),
        P("mlp"),
    )
    out_specs = P("req", None, "mlp")
    return jax.shard_map(
        on_device, mesh=mesh, in_specs=in_specs, out_specs=out_specs, check_vma=False
    )
```
